128 devices in a mesh: tm: 32 (over y, x, core), space: 4 (over z).
Axes of the slice: x: 4, y: 4, z: 4, core: 2. Of those that a mesh axis runs over, the one named last changes fastest.
Arguments:
- fields: bfloat16 [1024, 8, 32, 256], P('tm', None, 'space'), may hold values from -6 to 6
- conv_in: bfloat16 [64, 8, 3, 3], replicated, may hold values from -0.75 to 0.75
- conv_mid: bfloat16 [128, 64, 3, 3], replicated, may hold values from -0.25 to 0.25
- obs_gain: bfloat16 [8, 64, 128, 256], P('space'), may hold values from -0.0014648438 to 0.0014648438
- transition: float32 [256, 256], replicated, as said below
- back_gain: float32 [256, 256], replicated, as said below
- retain: float32 [1024, 256], P('tm'), may hold values from 0.5 to 1.03
Outputs:
- filtered: float32 [1024, 256], P(('tm', 'space'))
- smoothed: float32 [1024, 256], P(('tm', 'space'))
The draws below stay inside these ranges and needn't reach their ends.
Inputs may be any that keep to these rules, and one draw needn't show every extreme that they name: The spectral norm of transition is below one. The spectral norm of back_gain is below one.
All inputs are finite; a program needn't handle non-finite values.
Results may differ from the reference program's by a relative error of at most 0.0045.
Values may be sent and summed in bfloat16 or wider, within the bound.
No kernel may reach another device: no remote copies, remote signals or barrier semaphores. Data moves between devices by JAX's collectives and lax.ppermute only.
A program may use at most 192 MiB of HBM per device.

```python
import jax
import jax.numpy as jnp
from jax import lax

CH_IN = 8
C1 = 64
C2 = 128
PATTERN_COUNT = 256
HOUR_DEV = 32
LON = 256
CLOCK_SPAN = 1024
LAT = 32
LAT4 = 8
LON4 = 64
N_TM = 32


def decay_rates(key):
    key_slow, key_long, key_fast = jax.random.split(key, 3)
    share = 0.5
    is_slow = jax.random.bernoulli(key_slow, share, (PATTERN_COUNT // 2,))
    log_span = jax.random.uniform(key_long, (PATTERN_COUNT // 2,), jnp.float32, jnp.log(0.2), jnp.log(1.5))
    slow_rate = jnp.exp(-jnp.exp(log_span) / CLOCK_SPAN)
    fast_span = jax.random.uniform(key_fast, (PATTERN_COUNT // 2,), jnp.float32, 25.0, 50.0)
    fast_rate = jnp.exp(-1.0 / fast_span)
    return jnp.where(is_slow, slow_rate, fast_rate)


def rotation_mix(key, rates):
    key_turn, key_sign, key_mirror = jax.random.split(key, 3)
    magnitude = jax.random.uniform(key_turn, (PATTERN_COUNT // 2,), jnp.float32, 0.25, 1.0)
    flipped = jnp.where(jax.random.bernoulli(key_sign, 0.5, (PATTERN_COUNT // 2,)), 1.0, -1.0)
    angles = magnitude * flipped
    indices = jnp.arange(PATTERN_COUNT)
    pair_of = indices // 2
    parity = indices % 2
    same_pair = pair_of[:, None] == pair_of[None, :]
    radius = rates[pair_of][:, None]
    cosine = jnp.cos(angles)[pair_of][:, None]
    sine_part = jnp.sin(angles)[pair_of][:, None]
    on_diag = parity[:, None] == parity[None, :]
    off_part = jnp.where(parity[:, None] == 1, sine_part, -sine_part)
    rotated = jnp.where(same_pair, radius * jnp.where(on_diag, cosine, off_part), 0.0)
    mirror = jax.random.normal(key_mirror, (PATTERN_COUNT,), jnp.float32)
    length = jnp.sum(mirror * mirror)
    right_prod = jnp.sum(rotated * mirror[None, :], axis=1)
    left_prod = jnp.sum(mirror[:, None] * rotated, axis=0)
    middle = jnp.sum(mirror * right_prod)
    mixed = rotated - 2.0 / length * mirror[:, None] * left_prod[None, :]
    mixed = mixed - 2.0 / length * right_prod[:, None] * mirror[None, :]
    return mixed + 4.0 / (length * length) * middle * mirror[:, None] * mirror[None, :]


def draw_transition(key, part):
    return rotation_mix(jax.random.fold_in(key, 11), decay_rates(jax.random.fold_in(key, 12)))


def draw_back_gain(key, part):
    return rotation_mix(jax.random.fold_in(key, 21), decay_rates(jax.random.fold_in(key, 22)))


def draw_retain(key, part):
    storm_seed, amount_seed, level_seed = jax.random.split(jax.random.fold_in(key, 31), 3)
    storm_chance = 4.0 / CLOCK_SPAN
    storm_events = jax.random.uniform(storm_seed, (CLOCK_SPAN, PATTERN_COUNT), jnp.float32) < storm_chance
    water_amount = jax.random.uniform(amount_seed, (CLOCK_SPAN, PATTERN_COUNT), jnp.float32, 0.5, 0.8)
    drizzle_level = jax.random.uniform(level_seed, (CLOCK_SPAN, PATTERN_COUNT), jnp.float32, 0.97, 1.03)
    return jnp.where(storm_events, water_amount, drizzle_level)


def levels(key, dims, cuts, least, top_value):
    def one(dim, shards_of):
        heights = jax.random.uniform(jax.random.fold_in(jax.random.fold_in(key, 6), dim), (shards_of,), jnp.float32, least / len(cuts), top_value / len(cuts))
        return jnp.repeat(jnp.exp(heights), dims[dim] // shards_of).reshape((-1,) + (1,) * (len(dims) - dim - 1))

    loudness = one(*cuts[0])
    for cut in cuts[1:]:
        loudness = loudness * one(*cut)
    return loudness


def normal_values(rng, extent, scale, reach, pieces=(), held_as=jnp.bfloat16):
    values = jax.random.normal(rng, extent, jnp.float32) * scale
    if len(pieces) > 0:
        values = levels(rng, extent, pieces, -0.22, 0.18) * values
    return jnp.clip(values, min=-reach, max=reach).astype(held_as)


def setup_inputs(seed: int = 0) -> dict:
    streams_of = jax.random.split(jax.random.key(seed), 8)
    fields = normal_values(streams_of[0], (CLOCK_SPAN, CH_IN, LAT, LON), 1.0, 6.0, ((0, 32), (2, 4)))
    conv_in = normal_values(streams_of[1], (C1, CH_IN, 3, 3), (CH_IN * 9) ** -0.5, 0.75)
    conv_mid = normal_values(streams_of[2], (C2, C1, 3, 3), (C1 * 9) ** -0.5, 0.25)
    obs_gain = normal_values(streams_of[3], (LAT4, LON4, C2, PATTERN_COUNT), (LAT4 * LON4 * C2 * 256) ** -0.5, 0.0014648438, ((0, 4),))
    transition = draw_transition(jax.random.fold_in(streams_of[7], 71), 0)
    back_gain = draw_back_gain(jax.random.fold_in(streams_of[7], 71), 0)
    retain = draw_retain(jax.random.fold_in(streams_of[7], 71), 0)
    return {"fields": fields, "conv_in": conv_in, "conv_mid": conv_mid, "obs_gain": obs_gain, "transition": transition, "back_gain": back_gain, "retain": retain}


precise = lax.Precision.HIGHEST


def encode_block(block, conv_in, conv_mid, obs_gain):
    hidden = lax.conv_general_dilated(block, conv_in, (2, 2), ((1, 1), (1, 1)), dimension_numbers=("NCHW", "OIHW", "NCHW"), preferred_element_type=jnp.float32)
    hidden = jax.nn.silu(hidden).astype(jnp.bfloat16)
    encoded = lax.conv_general_dilated(hidden, conv_mid, (2, 2), ((1, 1), (1, 1)), dimension_numbers=("NCHW", "OIHW", "NHWC"), preferred_element_type=jnp.float32)
    encoded = jax.nn.silu(encoded).astype(jnp.bfloat16)
    return jnp.einsum("shwc,hwcm->sm", encoded.astype(jnp.float32), obs_gain.astype(jnp.float32))


def reference(fields, conv_in, conv_mid, obs_gain, transition, back_gain, retain):
    blocks = fields.reshape((N_TM, HOUR_DEV, CH_IN, LAT, LON))
    increments = lax.map(lambda block: encode_block(block, conv_in, conv_mid, obs_gain), blocks)
    increments = increments.reshape((CLOCK_SPAN, PATTERN_COUNT))

    def forward_step(state, inputs):
        gate_row, increment = inputs
        state = gate_row * jnp.dot(transition, state, precision=precise) + increment
        return state, state

    final_state, filtered = lax.scan(forward_step, jnp.zeros((PATTERN_COUNT,), jnp.float32), (retain, increments))
    joined = jnp.dot(back_gain, transition, precision=precise)
    sources = filtered - jnp.dot(filtered, joined.T, precision=precise)
    boundary = jnp.dot(transition, final_state, precision=precise)

    def back_step(state, source):
        state = source + jnp.dot(back_gain, state, precision=precise)
        return state, state

    first_state, smoothed = lax.scan(back_step, boundary, sources, reverse=True)
    return filtered, smoothed
```

```python
import jax
import jax.numpy as jnp
from jax import lax
from jax.sharding import PartitionSpec as P

precise = lax.Precision.HIGHEST
FLAT = ("tm", "space")


def dot(a, b):
    return jnp.dot(a, b, precision=precise)


def shift_down(value, axis, steps, count):
    return lax.ppermute(value, axis, [(i, i + steps) for i in range(count - steps)])


def shift_up(value, axis, steps, count):
    return lax.ppermute(value, axis, [(i + steps, i) for i in range(count - steps)])


def conv_stride(images, kernel, layout_out):
    return lax.conv_general_dilated(
        images,
        kernel,
        (2, 2),
        ((0, 0), (1, 1)),
        dimension_numbers=("NCHW", "OIHW", layout_out),
        preferred_element_type=jnp.float32,
    )


def encode(fields, conv_in, conv_mid, obs_gain, bands):
    band = lax.axis_index("space")
    above = shift_down(fields[:, :, -3:, :], "space", 1, bands)
    hidden = conv_stride(jnp.concatenate([above, fields], axis=2), conv_in, "NCHW")
    hidden = jax.nn.silu(hidden).astype(jnp.bfloat16)
    row = lax.broadcasted_iota(jnp.int32, hidden.shape, 2)
    hidden = jnp.where((row == 0) & (band == 0), jnp.zeros_like(hidden), hidden)
    encoded = conv_stride(hidden, conv_mid, "NHWC")
    encoded = jax.nn.silu(encoded).astype(jnp.bfloat16)
    return jnp.einsum("shwc,hwcm->sm", encoded, obs_gain, preferred_element_type=jnp.float32)


def scatter_bands(partial, bands):
    band = lax.axis_index("space")
    parts = partial.reshape((bands, partial.shape[0] // bands) + partial.shape[1:])
    total = lax.dynamic_index_in_dim(parts, band, 0, False)
    for step in range(1, bands):
        send = lax.dynamic_index_in_dim(parts, (band + step) % bands, 0, False)
        total = total + lax.ppermute(send, "space", [(i, (i + step) % bands) for i in range(bands)])
    return total


def per_device(fields, conv_in, conv_mid, obs_gain, transition, back_gain, retain):
    bands = lax.axis_size("space")
    count = lax.axis_size("tm") * bands
    place = lax.axis_index("tm") * bands + lax.axis_index("space")
    hours = fields.shape[0] // bands
    modes = transition.shape[0]

    gates = lax.dynamic_slice_in_dim(retain, lax.axis_index("space") * hours, hours, 0)
    transition_t = transition.T
    back_t = back_gain.T

    prefix = [gates[0][:, None] * transition]
    for i in range(1, hours):
        prefix.append(gates[i][:, None] * dot(transition, prefix[-1]))
    whole = prefix[-1]
    prefix = jnp.stack(prefix)

    partial = encode(fields, conv_in, conv_mid, obs_gain, bands)
    increments = scatter_bands(partial, bands)

    state = increments[0]
    local = [state]
    for i in range(1, hours):
        state = gates[i] * dot(state, transition_t) + increments[i]
        local.append(state)
    local = jnp.stack(local)
    summary = local[-1]

    mat1 = shift_down(whole, FLAT, 1, count)
    mat2 = shift_down(whole, FLAT, 2, count)
    vec1 = shift_down(summary, FLAT, 1, count)
    vec2 = shift_down(summary, FLAT, 2, count)
    carry = vec1 + dot(mat1, vec2)
    gain = dot(mat1, mat2)
    stride = 2
    while stride < count:
        got = shift_down(carry, FLAT, stride, count)
        if stride * 2 < count:
            got_gain = shift_down(gain, FLAT, stride, count)
        carry = carry + dot(gain, got)
        if stride * 2 < count:
            gain = dot(gain, got_gain)
        stride *= 2

    filtered = local + jnp.einsum("iab,b->ia", prefix, carry, precision=precise)

    powers = [jnp.eye(modes, dtype=jnp.float32), back_gain]
    for _ in range(2, hours + 1):
        powers.append(dot(back_gain, powers[-1]))
    joined_t = dot(back_gain, transition).T
    sources = filtered - dot(filtered, joined_t)
    stacked = jnp.concatenate([p.T for p in powers[:hours]], axis=0)
    padded = jnp.concatenate([sources, jnp.zeros_like(sources)], axis=0)
    hankel = jnp.concatenate([padded[d : d + hours] for d in range(hours)], axis=1)
    inner = dot(hankel, stacked)

    is_last = place == count - 1
    boundary = dot(transition, filtered[-1])
    head = inner[0] + jnp.where(is_last, dot(powers[hours], boundary), 0.0)

    step_power = powers[hours]
    got1 = shift_up(head, FLAT, 1, count)
    got2 = shift_up(head, FLAT, 2, count)
    entering = got1 + dot(step_power, got2)
    jump = dot(step_power, step_power)
    stride = 2
    while stride < count:
        got = shift_up(entering, FLAT, stride, count)
        entering = entering + dot(jump, got)
        jump = dot(jump, jump)
        stride *= 2
    entering = jnp.where(is_last, boundary, entering)

    tails = jnp.concatenate([powers[hours - i].T for i in range(hours)], axis=1)
    smoothed = inner + dot(entering[None, :], tails).reshape(hours, modes)
    return filtered, smoothed


def solution(mesh):
    placed = (
        P("tm", None, "space", None),
        P(),
        P(),
        P("space", None, None, None),
        P(),
        P(),
        P("tm", None),
    )
    return jax.shard_map(
        per_device,
        mesh=mesh,
        in_specs=placed,
        out_specs=(P(FLAT, None), P(FLAT, None)),
        check_vma=False,
    )
```

```python
import jax
import jax.numpy as jnp
from jax import lax
from jax.sharding import PartitionSpec as P

precise = lax.Precision.HIGHEST
FLAT = ("tm", "space")


def dot(a, b):
    return jnp.dot(a, b, precision=precise)


def shift_down(value, axis, steps, count):
    return lax.ppermute(value, axis, [(i, i + steps) for i in range(count - steps)])


def shift_up(value, axis, steps, count):
    return lax.ppermute(value, axis, [(i + steps, i) for i in range(count - steps)])


def conv_stride(images, kernel, layout_out):
    return lax.conv_general_dilated(
        images,
        kernel,
        (2, 2),
        ((0, 0), (1, 1)),
        dimension_numbers=("NCHW", "OIHW", layout_out),
        preferred_element_type=jnp.float32,
    )


def encode(fields, conv_in, conv_mid, obs_gain, bands):
    band = lax.axis_index("space")
    above = shift_down(fields[:, :, -3:, :], "space", 1, bands)
    hidden = conv_stride(jnp.concatenate([above, fields], axis=2), conv_in, "NCHW")
    hidden = jax.nn.silu(hidden).astype(jnp.bfloat16)
    row = lax.broadcasted_iota(jnp.int32, hidden.shape, 2)
    hidden = jnp.where((row == 0) & (band == 0), jnp.zeros_like(hidden), hidden)
    encoded = conv_stride(hidden, conv_mid, "NHWC")
    encoded = jax.nn.silu(encoded).astype(jnp.bfloat16)
    return jnp.einsum("shwc,hwcm->sm", encoded, obs_gain, preferred_element_type=jnp.float32)


def scatter_bands(partial, bands):
    band = lax.axis_index("space")
    parts = partial.reshape((bands, partial.shape[0] // bands) + partial.shape[1:])
    total = lax.dynamic_index_in_dim(parts, band, 0, False)
    for step in range(1, bands):
        send = lax.dynamic_index_in_dim(parts, (band + step) % bands, 0, False)
        total = total + lax.ppermute(send, "space", [(i, (i + step) % bands) for i in range(bands)])
    return total


def per_device(fields, conv_in, conv_mid, obs_gain, transition, back_gain, retain):
    bands = lax.axis_size("space")
    count = lax.axis_size("tm") * bands
    place = lax.axis_index("tm") * bands + lax.axis_index("space")
    hours = fields.shape[0] // bands
    modes = transition.shape[0]

    gates = lax.dynamic_slice_in_dim(retain, lax.axis_index("space") * hours, hours, 0)
    transition_t = transition.T
    back_t = back_gain.T

    prefix = [gates[0][:, None] * transition]
    for i in range(1, hours):
        prefix.append(gates[i][:, None] * dot(transition, prefix[-1]))
    whole = prefix[-1]
    prefix = jnp.stack(prefix)

    partial = encode(fields, conv_in, conv_mid, obs_gain, bands)
    increments = scatter_bands(partial, bands)

    state = increments[0]
    local = [state]
    for i in range(1, hours):
        state = gates[i] * dot(state, transition_t) + increments[i]
        local.append(state)
    local = jnp.stack(local)
    summary = local[-1]

    powers = [jnp.eye(modes, dtype=jnp.float32), back_gain]
    for _ in range(2, hours + 1):
        powers.append(dot(back_gain, powers[-1]))
    joined_t = dot(back_gain, transition).T
    stacked = jnp.concatenate([p.T for p in powers[:hours]], axis=0)
    spread = jnp.concatenate(powers[:hours], axis=1)
    step_power = powers[hours]

    kept = prefix - jnp.einsum("ab,ibc->iac", joined_t.T, prefix, precision=precise)
    reach = dot(spread, kept.reshape(hours * modes, modes))
    kept_local = local - dot(local, joined_t)
    offset = dot(kept_local.reshape(1, hours * modes), stacked)[0]

    is_last = place == count - 1
    closing = dot(step_power, transition)
    reach = jnp.where(is_last, reach + dot(closing, whole), reach)
    offset = jnp.where(is_last, offset + dot(closing, summary), offset)

    mat1 = shift_down(whole, FLAT, 1, count)
    mat2 = shift_down(whole, FLAT, 2, count)
    vec1 = shift_down(summary, FLAT, 1, count)
    vec2 = shift_down(summary, FLAT, 2, count)
    carry = vec1 + dot(mat1, vec2)
    gain = dot(mat1, mat2)

    right_mats = jnp.stack([whole, reach])
    right_vecs = jnp.stack([summary, offset])
    mats1 = shift_up(right_mats, FLAT, 1, count)
    mats2 = shift_up(right_mats, FLAT, 2, count)
    vecs1 = shift_up(right_vecs, FLAT, 1, count)
    vecs2 = shift_up(right_vecs, FLAT, 2, count)
    r_prod = dot(mats2[0], mats1[0])
    r_reach = mats1[1] + dot(step_power, dot(mats2[1], mats1[0]))
    r_sum = dot(mats2[0], vecs1[0]) + vecs2[0]
    r_off = vecs1[1] + dot(step_power, dot(mats2[1], vecs1[0]) + vecs2[1])
    r_pow = dot(step_power, step_power)

    stride = 2
    while stride < count:
        more = stride * 2 < count
        got = shift_down(carry, FLAT, stride, count)
        if more:
            got_gain = shift_down(gain, FLAT, stride, count)
        carry = carry + dot(gain, got)
        if more:
            gain = dot(gain, got_gain)

        far_mats = shift_up(jnp.stack([r_prod, r_reach]), FLAT, stride, count)
        far_vecs = shift_up(jnp.stack([r_sum, r_off]), FLAT, stride, count)
        new_off = r_off + dot(r_pow, dot(far_mats[1], r_sum) + far_vecs[1])
        new_reach = r_reach + dot(r_pow, dot(far_mats[1], r_prod))
        if more:
            r_sum = dot(far_mats[0], r_sum) + far_vecs[0]
            r_prod = dot(far_mats[0], r_prod)
            r_pow = dot(r_pow, r_pow)
        r_off, r_reach = new_off, new_reach
        stride *= 2

    filtered = local + jnp.einsum("iab,b->ia", prefix, carry, precision=precise)
    final = filtered[-1]
    entering = jnp.where(is_last, dot(transition, final), dot(r_reach, final) + r_off)

    sources = filtered - dot(filtered, joined_t)
    padded = jnp.concatenate([sources, jnp.zeros_like(sources)], axis=0)
    hankel = jnp.concatenate([padded[d : d + hours] for d in range(hours)], axis=1)
    inner = dot(hankel, stacked)
    tails = jnp.concatenate([powers[hours - i].T for i in range(hours)], axis=1)
    smoothed = inner + dot(entering[None, :], tails).reshape(hours, modes)
    return filtered, smoothed


def solution(mesh):
    placed = (
        P("tm", None, "space", None),
        P(),
        P(),
        P("space", None, None, None),
        P(),
        P(),
        P("tm", None),
    )
    return jax.shard_map(
        per_device,
        mesh=mesh,
        in_specs=placed,
        out_specs=(P(FLAT, None), P(FLAT, None)),
        check_vma=False,
    )
```

```python
import jax
import jax.numpy as jnp
from jax import lax
from jax.sharding import PartitionSpec as P

precise = lax.Precision.HIGHEST
FLAT = ("tm", "space")


def dot(a, b):
    return jnp.dot(a, b, precision=precise)


def shift_down(value, axis, steps, count):
    return lax.ppermute(value, axis, [(i, i + steps) for i in range(count - steps)])


def shift_up(value, axis, steps, count):
    return lax.ppermute(value, axis, [(i + steps, i) for i in range(count - steps)])


def conv_stride(images, kernel, layout_out):
    return lax.conv_general_dilated(
        images,
        kernel,
        (2, 2),
        ((0, 0), (1, 1)),
        dimension_numbers=("NCHW", "OIHW", layout_out),
        preferred_element_type=jnp.float32,
    )


def encode(fields, conv_in, conv_mid, obs_gain, bands):
    band = lax.axis_index("space")
    above = shift_down(fields[:, :, -3:, :], "space", 1, bands)
    hidden = conv_stride(jnp.concatenate([above, fields], axis=2), conv_in, "NCHW")
    hidden = jax.nn.silu(hidden).astype(jnp.bfloat16)
    row = lax.broadcasted_iota(jnp.int32, hidden.shape, 2)
    hidden = jnp.where((row == 0) & (band == 0), jnp.zeros_like(hidden), hidden)
    encoded = conv_stride(hidden, conv_mid, "NHWC")
    encoded = jax.nn.silu(encoded).astype(jnp.bfloat16)
    return jnp.einsum("shwc,hwcm->sm", encoded, obs_gain, preferred_element_type=jnp.float32)


def sum_bands(partial, bands):
    got = [lax.ppermute(partial, "space", [(i, (i + d) % bands) for i in range(bands)]) for d in (1, 2, 3)]
    return (partial + got[1]) + (got[2] + got[0])


def exclusive_scan(mats, vecs, axis, count):
    mat1 = shift_down(mats, axis, 1, count)
    mat2 = shift_down(mats, axis, 2, count)
    vec1 = shift_down(vecs, axis, 1, count)
    vec2 = shift_down(vecs, axis, 2, count)
    carry = vec1 + dot(mat1, vec2)
    gain = dot(mat1, mat2)
    stride = 2
    while stride < count:
        more = stride * 2 < count
        got = shift_down(carry, axis, stride, count)
        if more:
            got_gain = shift_down(gain, axis, stride, count)
        carry = carry + dot(gain, got)
        if more:
            gain = dot(gain, got_gain)
        stride *= 2
    return carry


def suffix_scan(heads, step_power, axis, count):
    got1 = shift_up(heads, axis, 1, count)
    got2 = shift_up(heads, axis, 2, count)
    entering = got1 + dot(step_power, got2)
    jump = dot(step_power, step_power)
    stride = 2
    while stride < count:
        got = shift_up(entering, axis, stride, count)
        entering = entering + dot(jump, got)
        if stride * 2 < count:
            jump = dot(jump, jump)
        stride *= 2
    return entering


def per_device(fields, conv_in, conv_mid, obs_gain, transition, back_gain, retain):
    bands = lax.axis_size("space")
    blocks = lax.axis_size("tm")
    band = lax.axis_index("space")
    hours = fields.shape[0] // bands
    modes = transition.shape[0]
    gates = retain.reshape(bands, hours, modes)
    transition_t = transition.T

    current = gates[:, 0, :, None] * transition[None]
    prefix = [current]
    for i in range(1, hours):
        current = gates[:, i, :, None] * jnp.einsum("ab,sbc->sac", transition, current, precision=precise)
        prefix.append(current)
    prefix = jnp.stack(prefix, axis=1)
    phis = current
    block_phi = dot(dot(phis[3], phis[2]), dot(phis[1], phis[0])) if bands == 4 else None
    if block_phi is None:
        block_phi = phis[0]
        for s in range(1, bands):
            block_phi = dot(phis[s], block_phi)

    partial = encode(fields, conv_in, conv_mid, obs_gain, bands)
    increments = sum_bands(partial, bands).reshape(bands, hours, modes)

    state = increments[:, 0]
    local = [state]
    for i in range(1, hours):
        state = gates[:, i] * dot(state, transition_t) + increments[:, i]
        local.append(state)
    local = jnp.stack(local, axis=1)
    ends = local[:, -1]
    block_sum = ends[0]
    for s in range(1, bands):
        block_sum = dot(phis[s], block_sum) + ends[s]

    carry = exclusive_scan(block_phi, block_sum, "tm", blocks)
    starts = [carry]
    for s in range(bands - 1):
        starts.append(dot(phis[s], starts[-1]) + ends[s])
    starts = jnp.stack(starts)
    filtered = local + jnp.einsum("siab,sb->sia", prefix, starts, precision=precise)

    powers = [jnp.eye(modes, dtype=jnp.float32), back_gain]
    for _ in range(2, hours + 1):
        powers.append(dot(back_gain, powers[-1]))
    step = powers[hours]
    joined_t = dot(back_gain, transition).T
    stacked = jnp.concatenate([p.T for p in powers[:hours]], axis=0)
    sources = filtered - jnp.einsum("sia,ab->sib", filtered, joined_t, precision=precise)
    padded = jnp.concatenate([sources, jnp.zeros_like(sources)], axis=1)
    hankel = jnp.concatenate([padded[:, d : d + hours] for d in range(hours)], axis=2)
    inner = dot(hankel.reshape(bands * hours, hours * modes), stacked).reshape(bands, hours, modes)
    heads = inner[:, 0]
    block_head = heads[bands - 1]
    for s in range(bands - 2, -1, -1):
        block_head = heads[s] + dot(step, block_head)
    block_step = step
    for _ in range(bands - 1):
        block_step = dot(block_step, step)

    is_last = lax.axis_index("tm") == blocks - 1
    boundary = dot(transition, filtered[bands - 1, hours - 1])
    block_head = block_head + jnp.where(is_last, dot(block_step, boundary), 0.0)
    entering = suffix_scan(block_head, block_step, "tm", blocks)
    entering = jnp.where(is_last, boundary, entering)

    inputs = [entering]
    for s in range(bands - 1, 0, -1):
        inputs.insert(0, heads[s] + dot(step, inputs[0]))
    mine = lax.dynamic_index_in_dim(jnp.stack(inputs), band, 0, False)
    tails = jnp.concatenate([powers[hours - i].T for i in range(hours)], axis=1)
    smoothed = lax.dynamic_index_in_dim(inner, band, 0, False) + dot(mine[None, :], tails).reshape(hours, modes)
    return lax.dynamic_index_in_dim(filtered, band, 0, False), smoothed


def solution(mesh):
    placed = (
        P("tm", None, "space", None),
        P(),
        P(),
        P("space", None, None, None),
        P(),
        P(),
        P("tm", None),
    )
    return jax.shard_map(
        per_device,
        mesh=mesh,
        in_specs=placed,
        out_specs=(P(FLAT, None), P(FLAT, None)),
        check_vma=False,
    )
```

```python
import jax
import jax.numpy as jnp
from jax import lax
from jax.sharding import PartitionSpec as P

precise = lax.Precision.HIGHEST
FLAT = ("tm", "space")


def dot(a, b):
    return jnp.dot(a, b, precision=precise)


def shift_down(value, axis, steps, count):
    return lax.ppermute(value, axis, [(i, i + steps) for i in range(count - steps)])


def shift_up(value, axis, steps, count):
    return lax.ppermute(value, axis, [(i + steps, i) for i in range(count - steps)])


def conv_stride(images, kernel, layout_out):
    return lax.conv_general_dilated(
        images,
        kernel,
        (2, 2),
        ((0, 0), (1, 1)),
        dimension_numbers=("NCHW", "OIHW", layout_out),
        preferred_element_type=jnp.float32,
    )


def encode(fields, conv_in, conv_mid, obs_gain, bands):
    band = lax.axis_index("space")
    edge = fields[:, :, -3:, :]
    flat = edge.reshape(edge.shape[0] * edge.shape[1], edge.shape[2] * edge.shape[3])
    above = shift_down(flat, "space", 1, bands).reshape(edge.shape)
    hidden = conv_stride(jnp.concatenate([above, fields], axis=2), conv_in, "NCHW")
    hidden = jax.nn.silu(hidden).astype(jnp.bfloat16)
    row = lax.broadcasted_iota(jnp.int32, hidden.shape, 2)
    hidden = jnp.where((row == 0) & (band == 0), jnp.zeros_like(hidden), hidden)
    encoded = conv_stride(hidden, conv_mid, "NHWC")
    encoded = jax.nn.silu(encoded).astype(jnp.bfloat16)
    return jnp.einsum("shwc,hwcm->sm", encoded, obs_gain, preferred_element_type=jnp.float32)


def sum_bands(partial, bands):
    got = [lax.ppermute(partial, "space", [(i, (i + d) % bands) for i in range(bands)]) for d in (1, 2, 3)]
    return (partial + got[1]) + (got[2] + got[0])


def exclusive_scan(mats, vecs, axis, count):
    mat1 = shift_down(mats, axis, 1, count)
    mat2 = shift_down(mats, axis, 2, count)
    vec1 = shift_down(vecs, axis, 1, count)
    vec2 = shift_down(vecs, axis, 2, count)
    carry = vec1 + dot(mat1, vec2)
    gain = dot(mat1, mat2)
    stride = 2
    while stride < count:
        more = stride * 2 < count
        got = shift_down(carry, axis, stride, count)
        if more:
            got_gain = shift_down(gain, axis, stride, count)
        carry = carry + dot(gain, got)
        if more:
            gain = dot(gain, got_gain)
        stride *= 2
    return carry


def suffix_scan(heads, step_power, axis, count):
    got1 = shift_up(heads, axis, 1, count)
    got2 = shift_up(heads, axis, 2, count)
    entering = got1 + dot(step_power, got2)
    jump = dot(step_power, step_power)
    stride = 2
    while stride < count:
        got = shift_up(entering, axis, stride, count)
        entering = entering + dot(jump, got)
        if stride * 2 < count:
            jump = dot(jump, jump)
        stride *= 2
    return entering


def per_device(fields, conv_in, conv_mid, obs_gain, transition, back_gain, retain):
    bands = lax.axis_size("space")
    blocks = lax.axis_size("tm")
    band = lax.axis_index("space")
    hours = fields.shape[0] // bands
    modes = transition.shape[0]
    gates = retain.reshape(bands, hours, modes)
    transition_t = transition.T

    phis = gates[:, 0, :, None] * transition[None]
    for i in range(1, hours):
        phis = gates[:, i, :, None] * jnp.einsum("ab,sbc->sac", transition, phis, precision=precise)
    block_phi = phis[0]
    for s in range(1, bands):
        block_phi = dot(phis[s], block_phi)

    partial = encode(fields, conv_in, conv_mid, obs_gain, bands)
    increments = sum_bands(partial, bands).reshape(bands, hours, modes)

    state = increments[:, 0]
    local = [state]
    for i in range(1, hours):
        state = gates[:, i] * dot(state, transition_t) + increments[:, i]
        local.append(state)
    local = jnp.stack(local, axis=1)
    ends = local[:, -1]
    block_sum = ends[0]
    for s in range(1, bands):
        block_sum = dot(phis[s], block_sum) + ends[s]

    carry = exclusive_scan(block_phi, block_sum, "tm", blocks)
    starts = [carry]
    for s in range(bands - 1):
        starts.append(dot(phis[s], starts[-1]) + ends[s])
    state = jnp.stack(starts)
    filtered = []
    for i in range(hours):
        state = gates[:, i] * dot(state, transition_t) + increments[:, i]
        filtered.append(state)
    filtered = jnp.stack(filtered, axis=1)

    powers = [jnp.eye(modes, dtype=jnp.float32), back_gain]
    while len(powers) <= hours:
        top = powers[-1]
        more = jnp.einsum("ab,sbc->sac", top, jnp.stack(powers[1:]), precision=precise)
        powers.extend(list(more))
    powers = powers[: hours + 1]
    step = powers[hours]
    joined_t = dot(back_gain, transition).T
    stacked = jnp.concatenate([p.T for p in powers[:hours]], axis=0)
    sources = filtered - jnp.einsum("sia,ab->sib", filtered, joined_t, precision=precise)
    padded = jnp.concatenate([sources, jnp.zeros_like(sources)], axis=1)
    hankel = jnp.concatenate([padded[:, d : d + hours] for d in range(hours)], axis=2)
    inner = dot(hankel.reshape(bands * hours, hours * modes), stacked).reshape(bands, hours, modes)
    heads = inner[:, 0]
    block_head = heads[bands - 1]
    for s in range(bands - 2, -1, -1):
        block_head = heads[s] + dot(step, block_head)
    block_step = step
    reach = 1
    while reach < bands:
        block_step = dot(block_step, block_step)
        reach *= 2

    is_last = lax.axis_index("tm") == blocks - 1
    boundary = dot(transition, filtered[bands - 1, hours - 1])
    block_head = block_head + jnp.where(is_last, dot(block_step, boundary), 0.0)
    entering = suffix_scan(block_head, block_step, "tm", blocks)
    entering = jnp.where(is_last, boundary, entering)

    inputs = [entering]
    for s in range(bands - 1, 0, -1):
        inputs.insert(0, heads[s] + dot(step, inputs[0]))
    mine = lax.dynamic_index_in_dim(jnp.stack(inputs), band, 0, False)
    tails = jnp.concatenate([powers[hours - i].T for i in range(hours)], axis=1)
    smoothed = lax.dynamic_index_in_dim(inner, band, 0, False) + dot(mine[None, :], tails).reshape(hours, modes)
    return lax.dynamic_index_in_dim(filtered, band, 0, False), smoothed


def solution(mesh):
    placed = (
        P("tm", None, "space", None),
        P(),
        P(),
        P("space", None, None, None),
        P(),
        P(),
        P("tm", None),
    )
    return jax.shard_map(
        per_device,
        mesh=mesh,
        in_specs=placed,
        out_specs=(P(FLAT, None), P(FLAT, None)),
        check_vma=False,
    )
```

```python
import jax
import jax.numpy as jnp
from jax import lax
from jax.sharding import PartitionSpec as P

precise = lax.Precision.HIGHEST
FLAT = ("tm", "space")


def dot(a, b):
    return jnp.dot(a, b, precision=precise)


def shift_down(value, axis, steps, count):
    return lax.ppermute(value, axis, [(i, i + steps) for i in range(count - steps)])


def shift_up(value, axis, steps, count):
    return lax.ppermute(value, axis, [(i + steps, i) for i in range(count - steps)])


def conv_stride(images, kernel, layout_out):
    return lax.conv_general_dilated(
        images,
        kernel,
        (2, 2),
        ((0, 0), (1, 1)),
        dimension_numbers=("NCHW", "OIHW", layout_out),
        preferred_element_type=jnp.float32,
    )


def encode(fields, conv_in, conv_mid, obs_gain, bands):
    band = lax.axis_index("space")
    edge = fields[:, :, -3:, :]
    flat = edge.reshape(edge.shape[0] * edge.shape[1], edge.shape[2] * edge.shape[3])
    above = shift_down(flat, "space", 1, bands).reshape(edge.shape)
    hidden = conv_stride(jnp.concatenate([above, fields], axis=2), conv_in, "NCHW")
    hidden = jax.nn.silu(hidden).astype(jnp.bfloat16)
    row = lax.broadcasted_iota(jnp.int32, hidden.shape, 2)
    hidden = jnp.where((row == 0) & (band == 0), jnp.zeros_like(hidden), hidden)
    encoded = conv_stride(hidden, conv_mid, "NHWC")
    encoded = jax.nn.silu(encoded).astype(jnp.bfloat16)
    return jnp.einsum("shwc,hwcm->sm", encoded, obs_gain, preferred_element_type=jnp.float32)


def sum_bands(partial, bands):
    got = [lax.ppermute(partial, "space", [(i, (i + d) % bands) for i in range(bands)]) for d in (1, 2, 3)]
    return (partial + got[1]) + (got[2] + got[0])


def scan_gains(mats, axis, count):
    mat1 = shift_down(mats, axis, 1, count)
    mat2 = shift_down(mats, axis, 2, count)
    gains = [dot(mat1, mat2)]
    stride = 2
    while stride * 2 < count:
        got_gain = shift_down(gains[-1], axis, stride, count)
        gains.append(dot(gains[-1], got_gain))
        stride *= 2
    return mat1, gains


def scan_carry(mat1, gains, vecs, axis, count):
    vec1 = shift_down(vecs, axis, 1, count)
    vec2 = shift_down(vecs, axis, 2, count)
    carry = vec1 + dot(mat1, vec2)
    stride = 2
    for gain in gains:
        got = shift_down(carry, axis, stride, count)
        carry = carry + dot(gain, got)
        stride *= 2
    return carry


def suffix_scan(heads, step_power, axis, count):
    got1 = shift_up(heads, axis, 1, count)
    got2 = shift_up(heads, axis, 2, count)
    entering = got1 + dot(step_power, got2)
    jump = dot(step_power, step_power)
    stride = 2
    while stride < count:
        got = shift_up(entering, axis, stride, count)
        entering = entering + dot(jump, got)
        if stride * 2 < count:
            jump = dot(jump, jump)
        stride *= 2
    return entering


def per_device(fields, conv_in, conv_mid, obs_gain, transition, back_gain, retain):
    bands = lax.axis_size("space")
    blocks = lax.axis_size("tm")
    band = lax.axis_index("space")
    hours = fields.shape[0] // bands
    modes = transition.shape[0]
    gates = retain.reshape(bands, hours, modes)
    transition_t = transition.T

    phis = gates[:, 0, :, None] * transition[None]
    for i in range(1, hours):
        phis = gates[:, i, :, None] * jnp.einsum("ab,sbc->sac", transition, phis, precision=precise)
    block_phi = phis[0]
    for s in range(1, bands):
        block_phi = dot(phis[s], block_phi)

    mat1, gains = scan_gains(block_phi, "tm", blocks)
    partial = encode(fields, conv_in, conv_mid, obs_gain, bands)
    (mat1, gains), partial = lax.optimization_barrier(((mat1, gains), partial))
    increments = sum_bands(partial, bands).reshape(bands, hours, modes)

    state = increments[:, 0]
    local = [state]
    for i in range(1, hours):
        state = gates[:, i] * dot(state, transition_t) + increments[:, i]
        local.append(state)
    local = jnp.stack(local, axis=1)
    ends = local[:, -1]
    block_sum = ends[0]
    for s in range(1, bands):
        block_sum = dot(phis[s], block_sum) + ends[s]

    carry = scan_carry(mat1, gains, block_sum, "tm", blocks)
    starts = [carry]
    for s in range(bands - 1):
        starts.append(dot(phis[s], starts[-1]) + ends[s])
    state = jnp.stack(starts)
    filtered = []
    for i in range(hours):
        state = gates[:, i] * dot(state, transition_t) + increments[:, i]
        filtered.append(state)
    filtered = jnp.stack(filtered, axis=1)

    powers = [jnp.eye(modes, dtype=jnp.float32), back_gain]
    while len(powers) <= hours:
        top = powers[-1]
        more = jnp.einsum("ab,sbc->sac", top, jnp.stack(powers[1:]), precision=precise)
        powers.extend(list(more))
    powers = powers[: hours + 1]
    step = powers[hours]
    joined_t = dot(back_gain, transition).T
    stacked = jnp.concatenate([p.T for p in powers[:hours]], axis=0)
    sources = filtered - jnp.einsum("sia,ab->sib", filtered, joined_t, precision=precise)
    padded = jnp.concatenate([sources, jnp.zeros_like(sources)], axis=1)
    hankel = jnp.concatenate([padded[:, d : d + hours] for d in range(hours)], axis=2)
    inner = dot(hankel.reshape(bands * hours, hours * modes), stacked).reshape(bands, hours, modes)
    heads = inner[:, 0]
    block_head = heads[bands - 1]
    for s in range(bands - 2, -1, -1):
        block_head = heads[s] + dot(step, block_head)
    block_step = step
    reach = 1
    while reach < bands:
        block_step = dot(block_step, block_step)
        reach *= 2

    is_last = lax.axis_index("tm") == blocks - 1
    boundary = dot(transition, filtered[bands - 1, hours - 1])
    block_head = block_head + jnp.where(is_last, dot(block_step, boundary), 0.0)
    entering = suffix_scan(block_head, block_step, "tm", blocks)
    entering = jnp.where(is_last, boundary, entering)

    inputs = [entering]
    for s in range(bands - 1, 0, -1):
        inputs.insert(0, heads[s] + dot(step, inputs[0]))
    mine = lax.dynamic_index_in_dim(jnp.stack(inputs), band, 0, False)
    tails = jnp.concatenate([powers[hours - i].T for i in range(hours)], axis=1)
    smoothed = lax.dynamic_index_in_dim(inner, band, 0, False) + dot(mine[None, :], tails).reshape(hours, modes)
    return lax.dynamic_index_in_dim(filtered, band, 0, False), smoothed


def solution(mesh):
    placed = (
        P("tm", None, "space", None),
        P(),
        P(),
        P("space", None, None, None),
        P(),
        P(),
        P("tm", None),
    )
    return jax.shard_map(
        per_device,
        mesh=mesh,
        in_specs=placed,
        out_specs=(P(FLAT, None), P(FLAT, None)),
        check_vma=False,
    )
```

```python
import jax
import jax.numpy as jnp
from jax import lax
from jax.sharding import PartitionSpec as P

precise = lax.Precision.HIGHEST
FLAT = ("tm", "space")


def dot(a, b):
    return jnp.dot(a, b, precision=precise)


def shift_down(value, axis, steps, count):
    return lax.ppermute(value, axis, [(i, i + steps) for i in range(count - steps)])


def shift_up(value, axis, steps, count):
    return lax.ppermute(value, axis, [(i + steps, i) for i in range(count - steps)])


def conv_stride(images, kernel, layout_in, layout_out):
    return lax.conv_general_dilated(
        images,
        kernel,
        (2, 2),
        ((0, 0), (1, 1)),
        dimension_numbers=(layout_in, "OIHW", layout_out),
        preferred_element_type=jnp.float32,
    )


def encode(fields, conv_in, conv_mid, obs_gain, bands):
    band = lax.axis_index("space")
    rows = jnp.transpose(fields, (2, 3, 1, 0))
    above = shift_down(rows[-3:], "space", 1, bands)
    hidden = conv_stride(jnp.concatenate([above, rows], axis=0), conv_in, "HWCN", "NCHW")
    hidden = jax.nn.silu(hidden).astype(jnp.bfloat16)
    row = lax.broadcasted_iota(jnp.int32, hidden.shape, 2)
    hidden = jnp.where((row == 0) & (band == 0), jnp.zeros_like(hidden), hidden)
    encoded = conv_stride(hidden, conv_mid, "NCHW", "NHWC")
    encoded = jax.nn.silu(encoded).astype(jnp.bfloat16)
    return jnp.einsum("shwc,hwcm->sm", encoded, obs_gain, preferred_element_type=jnp.float32)


def sum_bands(partial, bands):
    got = [lax.ppermute(partial, "space", [(i, (i + d) % bands) for i in range(bands)]) for d in (1, 2, 3)]
    return (partial + got[1]) + (got[2] + got[0])


def exclusive_scan(mats, vecs, axis, count):
    mat1 = shift_down(mats, axis, 1, count)
    mat2 = shift_down(mats, axis, 2, count)
    vec1 = shift_down(vecs, axis, 1, count)
    vec2 = shift_down(vecs, axis, 2, count)
    carry = vec1 + dot(mat1, vec2)
    gain = dot(mat1, mat2)
    stride = 2
    while stride < count:
        more = stride * 2 < count
        got = shift_down(carry, axis, stride, count)
        if more:
            got_gain = shift_down(gain, axis, stride, count)
        carry = carry + dot(gain, got)
        if more:
            gain = dot(gain, got_gain)
        stride *= 2
    return carry


def suffix_scan(heads, step_power, axis, count):
    first = min(4, count - 1)
    got = [shift_up(heads, axis, m, count) for m in range(1, first + 1)]
    scales = [step_power]
    while len(scales) < first - 1:
        scales.append(dot(scales[-1], step_power))
    entering = got[0]
    if first > 1:
        entering = entering + dot(jnp.concatenate(scales[: first - 1], axis=1), jnp.concatenate(got[1:]))
    power = dot(scales[first - 2], step_power) if first > 1 else step_power
    window = first
    while window < count - 1:
        need = min(3, -(-(count - 1) // window) - 1)
        got = [shift_up(entering, axis, m * window, count) for m in range(1, need + 1)]
        scales = [power]
        while len(scales) < need:
            scales.append(dot(scales[-1], power))
        entering = entering + dot(jnp.concatenate(scales, axis=1), jnp.concatenate(got))
        window *= need + 1
        if window < count - 1:
            power = dot(scales[-1], power)
    return entering


def per_device(fields, conv_in, conv_mid, obs_gain, transition, back_gain, retain):
    bands = lax.axis_size("space")
    blocks = lax.axis_size("tm")
    band = lax.axis_index("space")
    hours = fields.shape[0] // bands
    modes = transition.shape[0]
    gates = retain.reshape(bands, hours, modes)
    transition_t = transition.T

    phis = gates[:, 0, :, None] * transition[None]
    for i in range(1, hours):
        phis = gates[:, i, :, None] * jnp.einsum("ab,sbc->sac", transition, phis, precision=precise)
    block_phi = phis[0]
    for s in range(1, bands):
        block_phi = dot(phis[s], block_phi)

    partial = encode(fields, conv_in, conv_mid, obs_gain, bands)
    increments = sum_bands(partial, bands).reshape(bands, hours, modes)

    state = increments[:, 0]
    local = [state]
    for i in range(1, hours):
        state = gates[:, i] * dot(state, transition_t) + increments[:, i]
        local.append(state)
    local = jnp.stack(local, axis=1)
    ends = local[:, -1]
    block_sum = ends[0]
    for s in range(1, bands):
        block_sum = dot(phis[s], block_sum) + ends[s]

    carry = exclusive_scan(block_phi, block_sum, "tm", blocks)
    starts = [carry]
    for s in range(bands - 1):
        starts.append(dot(phis[s], starts[-1]) + ends[s])
    state = jnp.stack(starts)
    filtered = []
    for i in range(hours):
        state = gates[:, i] * dot(state, transition_t) + increments[:, i]
        filtered.append(state)
    filtered = jnp.stack(filtered, axis=1)

    powers = [jnp.eye(modes, dtype=jnp.float32), back_gain]
    while len(powers) <= hours:
        top = powers[-1]
        more = jnp.einsum("ab,sbc->sac", top, jnp.stack(powers[1:]), precision=precise)
        powers.extend(list(more))
    powers = powers[: hours + 1]
    step = powers[hours]
    joined_t = dot(back_gain, transition).T
    stacked = jnp.concatenate([p.T for p in powers[:hours]], axis=0)
    sources = filtered - jnp.einsum("sia,ab->sib", filtered, joined_t, precision=precise)
    padded = jnp.concatenate([sources, jnp.zeros_like(sources)], axis=1)
    hankel = jnp.concatenate([padded[:, d : d + hours] for d in range(hours)], axis=2)
    inner = dot(hankel.reshape(bands * hours, hours * modes), stacked).reshape(bands, hours, modes)
    heads = inner[:, 0]
    block_head = heads[bands - 1]
    for s in range(bands - 2, -1, -1):
        block_head = heads[s] + dot(step, block_head)
    block_step = step
    reach = 1
    while reach < bands:
        block_step = dot(block_step, block_step)
        reach *= 2

    is_last = lax.axis_index("tm") == blocks - 1
    boundary = dot(transition, filtered[bands - 1, hours - 1])
    block_head = block_head + jnp.where(is_last, dot(block_step, boundary), 0.0)
    entering = suffix_scan(block_head, block_step, "tm", blocks)
    entering = jnp.where(is_last, boundary, entering)

    inputs = [entering]
    for s in range(bands - 1, 0, -1):
        inputs.insert(0, heads[s] + dot(step, inputs[0]))
    mine = lax.dynamic_index_in_dim(jnp.stack(inputs), band, 0, False)
    tails = jnp.concatenate([powers[hours - i].T for i in range(hours)], axis=1)
    smoothed = lax.dynamic_index_in_dim(inner, band, 0, False) + dot(mine[None, :], tails).reshape(hours, modes)
    return lax.dynamic_index_in_dim(filtered, band, 0, False), smoothed


def solution(mesh):
    placed = (
        P("tm", None, "space", None),
        P(),
        P(),
        P("space", None, None, None),
        P(),
        P(),
        P("tm", None),
    )
    return jax.shard_map(
        per_device,
        mesh=mesh,
        in_specs=placed,
        out_specs=(P(FLAT, None), P(FLAT, None)),
        check_vma=False,
    )
```

```python
import jax
import jax.numpy as jnp
from jax import lax
from jax.sharding import PartitionSpec as P

precise = lax.Precision.HIGHEST
FLAT = ("tm", "space")


def dot(a, b):
    return jnp.dot(a, b, precision=precise)


def shift_down(value, axis, steps, count):
    return lax.ppermute(value, axis, [(i, i + steps) for i in range(count - steps)])


def shift_up(value, axis, steps, count):
    return lax.ppermute(value, axis, [(i + steps, i) for i in range(count - steps)])


def conv_stride(images, kernel, layout_out):
    return lax.conv_general_dilated(
        images,
        kernel,
        (2, 2),
        ((0, 0), (1, 1)),
        dimension_numbers=("NCHW", "OIHW", layout_out),
        preferred_element_type=jnp.float32,
    )


def encode(fields, conv_in, conv_mid, obs_gain, bands):
    band = lax.axis_index("space")
    edge = fields[:, :, -3:, :]
    flat = edge.reshape(edge.shape[0] * edge.shape[1], edge.shape[2] * edge.shape[3])
    above = shift_down(flat, "space", 1, bands).reshape(edge.shape)
    hidden = conv_stride(jnp.concatenate([above, fields], axis=2), conv_in, "NCHW")
    hidden = jax.nn.silu(hidden).astype(jnp.bfloat16)
    row = lax.broadcasted_iota(jnp.int32, hidden.shape, 2)
    hidden = jnp.where((row == 0) & (band == 0), jnp.zeros_like(hidden), hidden)
    encoded = conv_stride(hidden, conv_mid, "NHWC")
    encoded = jax.nn.silu(encoded).astype(jnp.bfloat16)
    return jnp.einsum("shwc,hwcm->sm", encoded, obs_gain, preferred_element_type=jnp.float32)


def sum_bands(partial, bands):
    got = [lax.ppermute(partial, "space", [(i, (i + d) % bands) for i in range(bands)]) for d in (1, 2, 3)]
    return (partial + got[1]) + (got[2] + got[0])


def exclusive_scan(mats, vecs, axis, count):
    mat1 = shift_down(mats, axis, 1, count)
    mat2 = shift_down(mats, axis, 2, count)
    vec1 = shift_down(vecs, axis, 1, count)
    vec2 = shift_down(vecs, axis, 2, count)
    carry = vec1 + dot(mat1, vec2)
    gain = dot(mat1, mat2)
    stride = 2
    while stride < count:
        more = stride * 2 < count
        got = shift_down(carry, axis, stride, count)
        if more:
            got_gain = shift_down(gain, axis, stride, count)
        carry = carry + dot(gain, got)
        if more:
            gain = dot(gain, got_gain)
        stride *= 2
    return carry


def suffix_scan(heads, step_power, axis, count):
    got1 = shift_up(heads, axis, 1, count)
    got2 = shift_up(heads, axis, 2, count)
    entering = got1 + dot(step_power, got2)
    jump = dot(step_power, step_power)
    stride = 2
    while stride < count:
        got = shift_up(entering, axis, stride, count)
        entering = entering + dot(jump, got)
        if stride * 2 < count:
            jump = dot(jump, jump)
        stride *= 2
    return entering


def per_device(fields, conv_in, conv_mid, obs_gain, transition, back_gain, retain):
    bands = lax.axis_size("space")
    blocks = lax.axis_size("tm")
    band = lax.axis_index("space")
    hours = fields.shape[0] // bands
    modes = transition.shape[0]
    gates = retain.reshape(bands, hours, modes)
    transition_t = transition.T

    phis = gates[:, :, :, None] * transition[None, None]
    while phis.shape[1] > 1:
        phis = jnp.einsum("sjab,sjbc->sjac", phis[:, 1::2], phis[:, 0::2], precision=precise)
    phis = phis[:, 0]
    block_phi = phis[0]
    for s in range(1, bands):
        block_phi = dot(phis[s], block_phi)

    partial = encode(fields, conv_in, conv_mid, obs_gain, bands)
    increments = sum_bands(partial, bands).reshape(bands, hours, modes)

    state = increments[:, 0]
    local = [state]
    for i in range(1, hours):
        state = gates[:, i] * dot(state, transition_t) + increments[:, i]
        local.append(state)
    local = jnp.stack(local, axis=1)
    ends = local[:, -1]
    block_sum = ends[0]
    for s in range(1, bands):
        block_sum = dot(phis[s], block_sum) + ends[s]

    carry = exclusive_scan(block_phi, block_sum, "tm", blocks)
    starts = [carry]
    for s in range(bands - 1):
        starts.append(dot(phis[s], starts[-1]) + ends[s])
    state = jnp.stack(starts)
    filtered = []
    for i in range(hours):
        state = gates[:, i] * dot(state, transition_t) + increments[:, i]
        filtered.append(state)
    filtered = jnp.stack(filtered, axis=1)

    powers = [jnp.eye(modes, dtype=jnp.float32), back_gain]
    while len(powers) <= hours:
        top = powers[-1]
        more = jnp.einsum("ab,sbc->sac", top, jnp.stack(powers[1:]), precision=precise)
        powers.extend(list(more))
    powers = powers[: hours + 1]
    step = powers[hours]
    joined_t = dot(back_gain, transition).T
    stacked = jnp.concatenate([p.T for p in powers[:hours]], axis=0)
    sources = filtered - jnp.einsum("sia,ab->sib", filtered, joined_t, precision=precise)
    padded = jnp.concatenate([sources, jnp.zeros_like(sources)], axis=1)
    hankel = jnp.concatenate([padded[:, d : d + hours] for d in range(hours)], axis=2)
    inner = dot(hankel.reshape(bands * hours, hours * modes), stacked).reshape(bands, hours, modes)
    heads = inner[:, 0]
    strides = [powers[0], step]
    while len(strides) < bands:
        strides.append(dot(strides[-1], step))
    block_head = dot(jnp.concatenate(strides[:bands], axis=1), heads.reshape(bands * modes))
    block_step = step
    reach = 1
    while reach < bands:
        block_step = dot(block_step, block_step)
        reach *= 2

    is_last = lax.axis_index("tm") == blocks - 1
    boundary = dot(transition, filtered[bands - 1, hours - 1])
    block_head = block_head + jnp.where(is_last, dot(block_step, boundary), 0.0)
    entering = suffix_scan(block_head, block_step, "tm", blocks)
    entering = jnp.where(is_last, boundary, entering)

    inputs = [entering]
    for s in range(bands - 1, 0, -1):
        inputs.insert(0, heads[s] + dot(step, inputs[0]))
    mine = lax.dynamic_index_in_dim(jnp.stack(inputs), band, 0, False)
    tails = jnp.concatenate([powers[hours - i].T for i in range(hours)], axis=1)
    smoothed = lax.dynamic_index_in_dim(inner, band, 0, False) + dot(mine[None, :], tails).reshape(hours, modes)
    return lax.dynamic_index_in_dim(filtered, band, 0, False), smoothed


def solution(mesh):
    placed = (
        P("tm", None, "space", None),
        P(),
        P(),
        P("space", None, None, None),
        P(),
        P(),
        P("tm", None),
    )
    return jax.shard_map(
        per_device,
        mesh=mesh,
        in_specs=placed,
        out_specs=(P(FLAT, None), P(FLAT, None)),
        check_vma=False,
    )
```

```python
import jax
import jax.numpy as jnp
from jax import lax
from jax.sharding import PartitionSpec as P

precise = lax.Precision.HIGHEST
FLAT = ("tm", "space")


def dot(a, b):
    return jnp.dot(a, b, precision=precise)


def shift_down(value, axis, steps, count):
    return lax.ppermute(value, axis, [(i, i + steps) for i in range(count - steps)])


def shift_up(value, axis, steps, count):
    return lax.ppermute(value, axis, [(i + steps, i) for i in range(count - steps)])


def conv_stride(images, kernel, layout_out):
    return lax.conv_general_dilated(
        images,
        kernel,
        (2, 2),
        ((0, 0), (1, 1)),
        dimension_numbers=("NCHW", "OIHW", layout_out),
        preferred_element_type=jnp.float32,
    )


def halo(fields, bands):
    edge = fields[:, :, -3:, :]
    flat = edge.reshape(edge.shape[0] * edge.shape[1], edge.shape[2] * edge.shape[3])
    return shift_down(flat, "space", 1, bands).reshape(edge.shape)


def encode(fields, above, conv_in, conv_mid, obs_gain, bands):
    band = lax.axis_index("space")
    hidden = conv_stride(jnp.concatenate([above, fields], axis=2), conv_in, "NCHW")
    hidden = jax.nn.silu(hidden).astype(jnp.bfloat16)
    row = lax.broadcasted_iota(jnp.int32, hidden.shape, 2)
    hidden = jnp.where((row == 0) & (band == 0), jnp.zeros_like(hidden), hidden)
    encoded = conv_stride(hidden, conv_mid, "NHWC")
    encoded = jax.nn.silu(encoded).astype(jnp.bfloat16)
    return jnp.einsum("shwc,hwcm->sm", encoded, obs_gain, preferred_element_type=jnp.float32)


def sum_bands(partial, bands):
    got = [lax.ppermute(partial, "space", [(i, (i + d) % bands) for i in range(bands)]) for d in (1, 2, 3)]
    return (partial + got[1]) + (got[2] + got[0])


def exclusive_scan(mats, vecs, axis, count):
    mat1 = shift_down(mats, axis, 1, count)
    mat2 = shift_down(mats, axis, 2, count)
    vec1 = shift_down(vecs, axis, 1, count)
    vec2 = shift_down(vecs, axis, 2, count)
    carry = vec1 + dot(mat1, vec2)
    gain = dot(mat1, mat2)
    stride = 2
    while stride < count:
        more = stride * 2 < count
        got = shift_down(carry, axis, stride, count)
        if more:
            got_gain = shift_down(gain, axis, stride, count)
        carry = carry + dot(gain, got)
        if more:
            gain = dot(gain, got_gain)
        stride *= 2
    return carry


def suffix_scan(heads, step_power, axis, count):
    got1 = shift_up(heads, axis, 1, count)
    got2 = shift_up(heads, axis, 2, count)
    entering = got1 + dot(step_power, got2)
    jump = dot(step_power, step_power)
    stride = 2
    while stride < count:
        got = shift_up(entering, axis, stride, count)
        entering = entering + dot(jump, got)
        if stride * 2 < count:
            jump = dot(jump, jump)
        stride *= 2
    return entering


def per_device(fields, conv_in, conv_mid, obs_gain, transition, back_gain, retain):
    bands = lax.axis_size("space")
    blocks = lax.axis_size("tm")
    band = lax.axis_index("space")
    hours = fields.shape[0] // bands
    modes = transition.shape[0]
    gates = retain.reshape(bands, hours, modes)
    transition_t = transition.T

    phis = gates[:, 0, :, None] * transition[None]
    for i in range(1, hours):
        phis = gates[:, i, :, None] * jnp.einsum("ab,sbc->sac", transition, phis, precision=precise)
    block_phi = phis[0]
    for s in range(1, bands):
        block_phi = dot(phis[s], block_phi)

    above = halo(fields, bands)
    above, block_phi = lax.optimization_barrier((above, block_phi))
    partial = encode(fields, above, conv_in, conv_mid, obs_gain, bands)
    increments = sum_bands(partial, bands).reshape(bands, hours, modes)

    state = increments[:, 0]
    local = [state]
    for i in range(1, hours):
        state = gates[:, i] * dot(state, transition_t) + increments[:, i]
        local.append(state)
    local = jnp.stack(local, axis=1)
    ends = local[:, -1]
    block_sum = ends[0]
    for s in range(1, bands):
        block_sum = dot(phis[s], block_sum) + ends[s]

    carry = exclusive_scan(block_phi, block_sum, "tm", blocks)
    starts = [carry]
    for s in range(bands - 1):
        starts.append(dot(phis[s], starts[-1]) + ends[s])
    state = jnp.stack(starts)
    filtered = []
    for i in range(hours):
        state = gates[:, i] * dot(state, transition_t) + increments[:, i]
        filtered.append(state)
    filtered = jnp.stack(filtered, axis=1)

    powers = [jnp.eye(modes, dtype=jnp.float32), back_gain]
    while len(powers) <= hours:
        top = powers[-1]
        more = jnp.einsum("ab,sbc->sac", top, jnp.stack(powers[1:]), precision=precise)
        powers.extend(list(more))
    powers = powers[: hours + 1]
    step = powers[hours]
    joined_t = dot(back_gain, transition).T
    stacked = jnp.concatenate([p.T for p in powers[:hours]], axis=0)
    sources = filtered - jnp.einsum("sia,ab->sib", filtered, joined_t, precision=precise)
    padded = jnp.concatenate([sources, jnp.zeros_like(sources)], axis=1)
    hankel = jnp.concatenate([padded[:, d : d + hours] for d in range(hours)], axis=2)
    inner = dot(hankel.reshape(bands * hours, hours * modes), stacked).reshape(bands, hours, modes)
    heads = inner[:, 0]
    block_head = heads[bands - 1]
    for s in range(bands - 2, -1, -1):
        block_head = heads[s] + dot(step, block_head)
    block_step = step
    reach = 1
    while reach < bands:
        block_step = dot(block_step, block_step)
        reach *= 2

    is_last = lax.axis_index("tm") == blocks - 1
    boundary = dot(transition, filtered[bands - 1, hours - 1])
    block_head = block_head + jnp.where(is_last, dot(block_step, boundary), 0.0)
    entering = suffix_scan(block_head, block_step, "tm", blocks)
    entering = jnp.where(is_last, boundary, entering)

    inputs = [entering]
    for s in range(bands - 1, 0, -1):
        inputs.insert(0, heads[s] + dot(step, inputs[0]))
    mine = lax.dynamic_index_in_dim(jnp.stack(inputs), band, 0, False)
    tails = jnp.concatenate([powers[hours - i].T for i in range(hours)], axis=1)
    smoothed = lax.dynamic_index_in_dim(inner, band, 0, False) + dot(mine[None, :], tails).reshape(hours, modes)
    return lax.dynamic_index_in_dim(filtered, band, 0, False), smoothed


def solution(mesh):
    placed = (
        P("tm", None, "space", None),
        P(),
        P(),
        P("space", None, None, None),
        P(),
        P(),
        P("tm", None),
    )
    return jax.shard_map(
        per_device,
        mesh=mesh,
        in_specs=placed,
        out_specs=(P(FLAT, None), P(FLAT, None)),
        check_vma=False,
    )
```

```python
import jax
import jax.numpy as jnp
from jax import lax
from jax.sharding import PartitionSpec as P

precise = lax.Precision.HIGHEST
FLAT = ("tm", "space")


def dot(a, b):
    return jnp.dot(a, b, precision=precise)


def shift_down(value, axis, steps, count):
    return lax.ppermute(value, axis, [(i, i + steps) for i in range(count - steps)])


def shift_up(value, axis, steps, count):
    return lax.ppermute(value, axis, [(i + steps, i) for i in range(count - steps)])


def conv_stride(images, kernel, layout_out):
    return lax.conv_general_dilated(
        images,
        kernel,
        (2, 2),
        ((0, 0), (1, 1)),
        dimension_numbers=("NCHW", "OIHW", layout_out),
        preferred_element_type=jnp.float32,
    )


def halo(fields, bands):
    return shift_down(fields[:, :, -3:, :], "space", 1, bands)


def encode(fields, above, conv_in, conv_mid, obs_gain, bands):
    band = lax.axis_index("space")
    hidden = conv_stride(jnp.concatenate([above, fields], axis=2), conv_in, "NCHW")
    hidden = jax.nn.silu(hidden).astype(jnp.bfloat16)
    row = lax.broadcasted_iota(jnp.int32, hidden.shape, 2)
    hidden = jnp.where((row == 0) & (band == 0), jnp.zeros_like(hidden), hidden)
    encoded = conv_stride(hidden, conv_mid, "NHWC")
    encoded = jax.nn.silu(encoded).astype(jnp.bfloat16)
    return jnp.einsum("shwc,hwcm->sm", encoded, obs_gain, preferred_element_type=jnp.float32)


def sum_bands(partial, bands):
    got = [lax.ppermute(partial, "space", [(i, (i + d) % bands) for i in range(bands)]) for d in (1, 2, 3)]
    return (partial + got[1]) + (got[2] + got[0])


def exclusive_scan(mats, vecs, axis, count):
    mat1 = shift_down(mats, axis, 1, count)
    mat2 = shift_down(mats, axis, 2, count)
    vec1 = shift_down(vecs, axis, 1, count)
    vec2 = shift_down(vecs, axis, 2, count)
    carry = vec1 + dot(mat1, vec2)
    gain = dot(mat1, mat2)
    stride = 2
    while stride < count:
        more = stride * 2 < count
        got = shift_down(carry, axis, stride, count)
        if more:
            got_gain = shift_down(gain, axis, stride, count)
        carry = carry + dot(gain, got)
        if more:
            gain = dot(gain, got_gain)
        stride *= 2
    return carry


def suffix_scan(heads, step_power, axis, count):
    got1 = shift_up(heads, axis, 1, count)
    got2 = shift_up(heads, axis, 2, count)
    entering = got1 + dot(step_power, got2)
    jump = dot(step_power, step_power)
    stride = 2
    while stride < count:
        got = shift_up(entering, axis, stride, count)
        entering = entering + dot(jump, got)
        if stride * 2 < count:
            jump = dot(jump, jump)
        stride *= 2
    return entering


def per_device(fields, conv_in, conv_mid, obs_gain, transition, back_gain, retain):
    bands = lax.axis_size("space")
    blocks = lax.axis_size("tm")
    band = lax.axis_index("space")
    hours = fields.shape[0] // bands
    modes = transition.shape[0]
    gates = retain.reshape(bands, hours, modes)
    transition_t = transition.T

    phis = gates[:, 0, :, None] * transition[None]
    for i in range(1, hours):
        phis = gates[:, i, :, None] * jnp.einsum("ab,sbc->sac", transition, phis, precision=precise)
    block_phi = phis[0]
    for s in range(1, bands):
        block_phi = dot(phis[s], block_phi)

    above = halo(fields, bands)
    above, block_phi = lax.optimization_barrier((above, block_phi))
    partial = encode(fields, above, conv_in, conv_mid, obs_gain, bands)
    increments = sum_bands(partial, bands).reshape(bands, hours, modes)

    state = increments[:, 0]
    local = [state]
    for i in range(1, hours):
        state = gates[:, i] * dot(state, transition_t) + increments[:, i]
        local.append(state)
    local = jnp.stack(local, axis=1)
    ends = local[:, -1]
    block_sum = ends[0]
    for s in range(1, bands):
        block_sum = dot(phis[s], block_sum) + ends[s]

    carry = exclusive_scan(block_phi, block_sum, "tm", blocks)
    starts = [carry]
    for s in range(bands - 1):
        starts.append(dot(phis[s], starts[-1]) + ends[s])
    state = jnp.stack(starts)
    filtered = []
    for i in range(hours):
        state = gates[:, i] * dot(state, transition_t) + increments[:, i]
        filtered.append(state)
    filtered = jnp.stack(filtered, axis=1)

    powers = [jnp.eye(modes, dtype=jnp.float32), back_gain]
    while len(powers) <= hours:
        top = powers[-1]
        more = jnp.einsum("ab,sbc->sac", top, jnp.stack(powers[1:]), precision=precise)
        powers.extend(list(more))
    powers = powers[: hours + 1]
    step = powers[hours]
    joined_t = dot(back_gain, transition).T
    stacked = jnp.concatenate([p.T for p in powers[:hours]], axis=0)
    sources = filtered - jnp.einsum("sia,ab->sib", filtered, joined_t, precision=precise)
    padded = jnp.concatenate([sources, jnp.zeros_like(sources)], axis=1)
    hankel = jnp.concatenate([padded[:, d : d + hours] for d in range(hours)], axis=2)
    inner = dot(hankel.reshape(bands * hours, hours * modes), stacked).reshape(bands, hours, modes)
    heads = inner[:, 0]
    block_head = heads[bands - 1]
    for s in range(bands - 2, -1, -1):
        block_head = heads[s] + dot(step, block_head)
    block_step = step
    reach = 1
    while reach < bands:
        block_step = dot(block_step, block_step)
        reach *= 2

    is_last = lax.axis_index("tm") == blocks - 1
    boundary = dot(transition, filtered[bands - 1, hours - 1])
    block_head = block_head + jnp.where(is_last, dot(block_step, boundary), 0.0)
    entering = suffix_scan(block_head, block_step, "tm", blocks)
    entering = jnp.where(is_last, boundary, entering)

    inputs = [entering]
    for s in range(bands - 1, 0, -1):
        inputs.insert(0, heads[s] + dot(step, inputs[0]))
    mine = lax.dynamic_index_in_dim(jnp.stack(inputs), band, 0, False)
    tails = jnp.concatenate([powers[hours - i].T for i in range(hours)], axis=1)
    smoothed = lax.dynamic_index_in_dim(inner, band, 0, False) + dot(mine[None, :], tails).reshape(hours, modes)
    return lax.dynamic_index_in_dim(filtered, band, 0, False), smoothed


def solution(mesh):
    placed = (
        P("tm", None, "space", None),
        P(),
        P(),
        P("space", None, None, None),
        P(),
        P(),
        P("tm", None),
    )
    return jax.shard_map(
        per_device,
        mesh=mesh,
        in_specs=placed,
        out_specs=(P(FLAT, None), P(FLAT, None)),
        check_vma=False,
    )
```

```python
import jax
import jax.numpy as jnp
from jax import lax
from jax.sharding import PartitionSpec as P

precise = lax.Precision.HIGHEST
product = lax.Precision.HIGH
FLAT = ("tm", "space")


def dot(a, b):
    return jnp.dot(a, b, precision=precise)


def mat(a, b):
    return jnp.dot(a, b, precision=product)


def shift_down(value, axis, steps, count):
    return lax.ppermute(value, axis, [(i, i + steps) for i in range(count - steps)])


def shift_up(value, axis, steps, count):
    return lax.ppermute(value, axis, [(i + steps, i) for i in range(count - steps)])


def conv_stride(images, kernel, layout_out):
    return lax.conv_general_dilated(
        images,
        kernel,
        (2, 2),
        ((0, 0), (1, 1)),
        dimension_numbers=("NCHW", "OIHW", layout_out),
        preferred_element_type=jnp.float32,
    )


def halo(fields, bands):
    return shift_down(fields[:, :, -3:, :], "space", 1, bands)


def encode(fields, above, conv_in, conv_mid, obs_gain, bands):
    band = lax.axis_index("space")
    hidden = conv_stride(jnp.concatenate([above, fields], axis=2), conv_in, "NCHW")
    hidden = jax.nn.silu(hidden).astype(jnp.bfloat16)
    row = lax.broadcasted_iota(jnp.int32, hidden.shape, 2)
    hidden = jnp.where((row == 0) & (band == 0), jnp.zeros_like(hidden), hidden)
    encoded = conv_stride(hidden, conv_mid, "NHWC")
    encoded = jax.nn.silu(encoded).astype(jnp.bfloat16)
    return jnp.einsum("shwc,hwcm->sm", encoded, obs_gain, preferred_element_type=jnp.float32)


def sum_bands(partial, bands):
    got = [lax.ppermute(partial, "space", [(i, (i + d) % bands) for i in range(bands)]) for d in (1, 2, 3)]
    return (partial + got[1]) + (got[2] + got[0])


def exclusive_scan(mats, vecs, axis, count):
    mat1 = shift_down(mats, axis, 1, count)
    mat2 = shift_down(mats, axis, 2, count)
    vec1 = shift_down(vecs, axis, 1, count)
    vec2 = shift_down(vecs, axis, 2, count)
    carry = vec1 + dot(mat1, vec2)
    gain = mat(mat1, mat2)
    stride = 2
    while stride < count:
        more = stride * 2 < count
        got = shift_down(carry, axis, stride, count)
        if more:
            got_gain = shift_down(gain, axis, stride, count)
        carry = carry + dot(gain, got)
        if more:
            gain = mat(gain, got_gain)
        stride *= 2
    return carry


def suffix_scan(heads, step_power, axis, count):
    got1 = shift_up(heads, axis, 1, count)
    got2 = shift_up(heads, axis, 2, count)
    entering = got1 + dot(step_power, got2)
    jump = dot(step_power, step_power)
    stride = 2
    while stride < count:
        got = shift_up(entering, axis, stride, count)
        entering = entering + dot(jump, got)
        if stride * 2 < count:
            jump = dot(jump, jump)
        stride *= 2
    return entering


def per_device(fields, conv_in, conv_mid, obs_gain, transition, back_gain, retain):
    bands = lax.axis_size("space")
    blocks = lax.axis_size("tm")
    band = lax.axis_index("space")
    hours = fields.shape[0] // bands
    modes = transition.shape[0]
    gates = retain.reshape(bands, hours, modes)
    transition_t = transition.T

    phis = gates[:, 0, :, None] * transition[None]
    for i in range(1, hours):
        phis = gates[:, i, :, None] * jnp.einsum("ab,sbc->sac", transition, phis, precision=product)
    block_phi = phis[0]
    for s in range(1, bands):
        block_phi = mat(phis[s], block_phi)

    above = halo(fields, bands)
    above, block_phi = lax.optimization_barrier((above, block_phi))
    partial = encode(fields, above, conv_in, conv_mid, obs_gain, bands)
    increments = sum_bands(partial, bands).reshape(bands, hours, modes)

    state = increments[:, 0]
    local = [state]
    for i in range(1, hours):
        state = gates[:, i] * dot(state, transition_t) + increments[:, i]
        local.append(state)
    local = jnp.stack(local, axis=1)
    ends = local[:, -1]
    block_sum = ends[0]
    for s in range(1, bands):
        block_sum = dot(phis[s], block_sum) + ends[s]

    carry = exclusive_scan(block_phi, block_sum, "tm", blocks)
    starts = [carry]
    for s in range(bands - 1):
        starts.append(dot(phis[s], starts[-1]) + ends[s])
    state = jnp.stack(starts)
    filtered = []
    for i in range(hours):
        state = gates[:, i] * dot(state, transition_t) + increments[:, i]
        filtered.append(state)
    filtered = jnp.stack(filtered, axis=1)

    powers = [jnp.eye(modes, dtype=jnp.float32), back_gain]
    while len(powers) <= hours:
        top = powers[-1]
        more = jnp.einsum("ab,sbc->sac", top, jnp.stack(powers[1:]), precision=precise)
        powers.extend(list(more))
    powers = powers[: hours + 1]
    step = powers[hours]
    joined_t = dot(back_gain, transition).T
    stacked = jnp.concatenate([p.T for p in powers[:hours]], axis=0)
    sources = filtered - jnp.einsum("sia,ab->sib", filtered, joined_t, precision=precise)
    padded = jnp.concatenate([sources, jnp.zeros_like(sources)], axis=1)
    hankel = jnp.concatenate([padded[:, d : d + hours] for d in range(hours)], axis=2)
    inner = dot(hankel.reshape(bands * hours, hours * modes), stacked).reshape(bands, hours, modes)
    heads = inner[:, 0]
    block_head = heads[bands - 1]
    for s in range(bands - 2, -1, -1):
        block_head = heads[s] + dot(step, block_head)
    block_step = step
    reach = 1
    while reach < bands:
        block_step = dot(block_step, block_step)
        reach *= 2

    is_last = lax.axis_index("tm") == blocks - 1
    boundary = dot(transition, filtered[bands - 1, hours - 1])
    block_head = block_head + jnp.where(is_last, dot(block_step, boundary), 0.0)
    entering = suffix_scan(block_head, block_step, "tm", blocks)
    entering = jnp.where(is_last, boundary, entering)

    inputs = [entering]
    for s in range(bands - 1, 0, -1):
        inputs.insert(0, heads[s] + dot(step, inputs[0]))
    mine = lax.dynamic_index_in_dim(jnp.stack(inputs), band, 0, False)
    tails = jnp.concatenate([powers[hours - i].T for i in range(hours)], axis=1)
    smoothed = lax.dynamic_index_in_dim(inner, band, 0, False) + dot(mine[None, :], tails).reshape(hours, modes)
    return lax.dynamic_index_in_dim(filtered, band, 0, False), smoothed


def solution(mesh):
    placed = (
        P("tm", None, "space", None),
        P(),
        P(),
        P("space", None, None, None),
        P(),
        P(),
        P("tm", None),
    )
    return jax.shard_map(
        per_device,
        mesh=mesh,
        in_specs=placed,
        out_specs=(P(FLAT, None), P(FLAT, None)),
        check_vma=False,
    )
```

```python
import jax
import jax.numpy as jnp
from jax import lax
from jax.sharding import PartitionSpec as P

precise = lax.Precision.HIGHEST
FLAT = ("tm", "space")


def dot(a, b):
    return jnp.dot(a, b, precision=precise)


def shift_down(value, axis, steps, count):
    return lax.ppermute(value, axis, [(i, i + steps) for i in range(count - steps)])


def shift_up(value, axis, steps, count):
    return lax.ppermute(value, axis, [(i + steps, i) for i in range(count - steps)])


def conv_stride(images, kernel, layout_out):
    return lax.conv_general_dilated(
        images,
        kernel,
        (2, 2),
        ((0, 0), (1, 1)),
        dimension_numbers=("NCHW", "OIHW", layout_out),
        preferred_element_type=jnp.float32,
    )


def halo(fields, bands):
    return shift_down(fields[:, :, -3:, :], "space", 1, bands)


def encode(fields, above, conv_in, conv_mid, obs_gain, bands):
    band = lax.axis_index("space")
    hidden = conv_stride(jnp.concatenate([above, fields], axis=2), conv_in, "NCHW")
    hidden = jax.nn.silu(hidden).astype(jnp.bfloat16)
    row = lax.broadcasted_iota(jnp.int32, hidden.shape, 2)
    hidden = jnp.where((row == 0) & (band == 0), jnp.zeros_like(hidden), hidden)
    encoded = conv_stride(hidden, conv_mid, "NHWC")
    encoded = jax.nn.silu(encoded).astype(jnp.bfloat16)
    return jnp.einsum("shwc,hwcm->sm", encoded, obs_gain, preferred_element_type=jnp.float32)


def sum_bands(partial, bands):
    got = [lax.ppermute(partial, "space", [(i, (i + d) % bands) for i in range(bands)]) for d in (1, 2, 3)]
    return (partial + got[1]) + (got[2] + got[0])


def exclusive_scan(mats, vecs, axis, count):
    joint = jnp.concatenate([mats, vecs[None, :]], axis=0)
    got1 = shift_down(joint, axis, 1, count)
    got2 = shift_down(joint, axis, 2, count)
    mat1, vec1 = got1[:-1], got1[-1]
    mat2, vec2 = got2[:-1], got2[-1]
    carry = vec1 + dot(mat1, vec2)
    gain = dot(mat1, mat2)
    stride = 2
    while stride < count:
        more = stride * 2 < count
        got = shift_down(carry, axis, stride, count)
        if more:
            got_gain = shift_down(gain, axis, stride, count)
        carry = carry + dot(gain, got)
        if more:
            gain = dot(gain, got_gain)
        stride *= 2
    return carry


def suffix_scan(heads, step_power, axis, count):
    got1 = shift_up(heads, axis, 1, count)
    got2 = shift_up(heads, axis, 2, count)
    entering = got1 + dot(step_power, got2)
    jump = dot(step_power, step_power)
    stride = 2
    while stride < count:
        got = shift_up(entering, axis, stride, count)
        entering = entering + dot(jump, got)
        if stride * 2 < count:
            jump = dot(jump, jump)
        stride *= 2
    return entering


def per_device(fields, conv_in, conv_mid, obs_gain, transition, back_gain, retain):
    bands = lax.axis_size("space")
    blocks = lax.axis_size("tm")
    band = lax.axis_index("space")
    hours = fields.shape[0] // bands
    modes = transition.shape[0]
    gates = retain.reshape(bands, hours, modes)
    transition_t = transition.T

    phis = gates[:, 0, :, None] * transition[None]
    for i in range(1, hours):
        phis = gates[:, i, :, None] * jnp.einsum("ab,sbc->sac", transition, phis, precision=precise)
    block_phi = phis[0]
    for s in range(1, bands):
        block_phi = dot(phis[s], block_phi)

    above = halo(fields, bands)
    above, block_phi = lax.optimization_barrier((above, block_phi))
    partial = encode(fields, above, conv_in, conv_mid, obs_gain, bands)
    increments = sum_bands(partial, bands).reshape(bands, hours, modes)

    state = increments[:, 0]
    local = [state]
    for i in range(1, hours):
        state = gates[:, i] * dot(state, transition_t) + increments[:, i]
        local.append(state)
    local = jnp.stack(local, axis=1)
    ends = local[:, -1]
    block_sum = ends[0]
    for s in range(1, bands):
        block_sum = dot(phis[s], block_sum) + ends[s]

    carry = exclusive_scan(block_phi, block_sum, "tm", blocks)
    starts = [carry]
    for s in range(bands - 1):
        starts.append(dot(phis[s], starts[-1]) + ends[s])
    state = jnp.stack(starts)
    filtered = []
    for i in range(hours):
        state = gates[:, i] * dot(state, transition_t) + increments[:, i]
        filtered.append(state)
    filtered = jnp.stack(filtered, axis=1)

    powers = [jnp.eye(modes, dtype=jnp.float32), back_gain]
    while len(powers) <= hours:
        top = powers[-1]
        more = jnp.einsum("ab,sbc->sac", top, jnp.stack(powers[1:]), precision=precise)
        powers.extend(list(more))
    powers = powers[: hours + 1]
    step = powers[hours]
    joined_t = dot(back_gain, transition).T
    stacked = jnp.concatenate([p.T for p in powers[:hours]], axis=0)
    sources = filtered - jnp.einsum("sia,ab->sib", filtered, joined_t, precision=precise)
    padded = jnp.concatenate([sources, jnp.zeros_like(sources)], axis=1)
    hankel = jnp.concatenate([padded[:, d : d + hours] for d in range(hours)], axis=2)
    inner = dot(hankel.reshape(bands * hours, hours * modes), stacked).reshape(bands, hours, modes)
    heads = inner[:, 0]
    block_head = heads[bands - 1]
    for s in range(bands - 2, -1, -1):
        block_head = heads[s] + dot(step, block_head)
    block_step = step
    reach = 1
    while reach < bands:
        block_step = dot(block_step, block_step)
        reach *= 2

    is_last = lax.axis_index("tm") == blocks - 1
    boundary = dot(transition, filtered[bands - 1, hours - 1])
    block_head = block_head + jnp.where(is_last, dot(block_step, boundary), 0.0)
    entering = suffix_scan(block_head, block_step, "tm", blocks)
    entering = jnp.where(is_last, boundary, entering)

    inputs = [entering]
    for s in range(bands - 1, 0, -1):
        inputs.insert(0, heads[s] + dot(step, inputs[0]))
    mine = lax.dynamic_index_in_dim(jnp.stack(inputs), band, 0, False)
    tails = jnp.concatenate([powers[hours - i].T for i in range(hours)], axis=1)
    smoothed = lax.dynamic_index_in_dim(inner, band, 0, False) + dot(mine[None, :], tails).reshape(hours, modes)
    return lax.dynamic_index_in_dim(filtered, band, 0, False), smoothed


def solution(mesh):
    placed = (
        P("tm", None, "space", None),
        P(),
        P(),
        P("space", None, None, None),
        P(),
        P(),
        P("tm", None),
    )
    return jax.shard_map(
        per_device,
        mesh=mesh,
        in_specs=placed,
        out_specs=(P(FLAT, None), P(FLAT, None)),
        check_vma=False,
    )
```

```python
import jax
import jax.numpy as jnp
from jax import lax
from jax.sharding import PartitionSpec as P

precise = lax.Precision.HIGHEST
FLAT = ("tm", "space")


def dot(a, b):
    return jnp.dot(a, b, precision=precise)


def shift_down(value, axis, steps, count):
    return lax.ppermute(value, axis, [(i, i + steps) for i in range(count - steps)])


def shift_up(value, axis, steps, count):
    return lax.ppermute(value, axis, [(i + steps, i) for i in range(count - steps)])


def conv_stride(images, kernel, layout_out):
    return lax.conv_general_dilated(
        images,
        kernel,
        (2, 2),
        ((0, 0), (1, 1)),
        dimension_numbers=("NCHW", "OIHW", layout_out),
        preferred_element_type=jnp.float32,
    )


def halo(fields, bands):
    return shift_down(fields[:, :, -3:, :], "space", 1, bands)


def encode(fields, above, conv_in, conv_mid, obs_gain, bands):
    band = lax.axis_index("space")
    hidden = conv_stride(jnp.concatenate([above, fields], axis=2), conv_in, "NCHW")
    hidden = jax.nn.silu(hidden).astype(jnp.bfloat16)
    row = lax.broadcasted_iota(jnp.int32, hidden.shape, 2)
    hidden = jnp.where((row == 0) & (band == 0), jnp.zeros_like(hidden), hidden)
    encoded = conv_stride(hidden, conv_mid, "NHWC")
    encoded = jax.nn.silu(encoded).astype(jnp.bfloat16)
    return jnp.einsum("shwc,hwcm->sm", encoded, obs_gain, preferred_element_type=jnp.float32)


def sum_bands(partial, bands):
    got = [lax.ppermute(partial, "space", [(i, (i + d) % bands) for i in range(bands)]) for d in (1, 2, 3)]
    return (partial + got[1]) + (got[2] + got[0])


def exclusive_scan(mats, vecs, axis, count):
    mat1 = shift_down(mats, axis, 1, count)
    mat2 = shift_down(mats, axis, 2, count)
    vec1 = shift_down(vecs, axis, 1, count)
    vec2 = shift_down(vecs, axis, 2, count)
    carry = vec1 + dot(mat1, vec2)
    gain = dot(mat1, mat2)
    stride = 2
    while stride < count:
        more = stride * 2 < count
        got = shift_down(carry, axis, stride, count)
        if more:
            got_gain = shift_down(gain, axis, stride, count)
        carry = carry + dot(gain, got)
        if more:
            gain = dot(gain, got_gain)
        stride *= 2
    return carry


def suffix_scan(heads, step_power, axis, count):
    got1 = shift_up(heads, axis, 1, count)
    got2 = shift_up(heads, axis, 2, count)
    entering = got1 + dot(step_power, got2)
    got2, jump = lax.optimization_barrier((got2, step_power))
    jump = dot(jump, jump)
    stride = 2
    while stride < count:
        got = shift_up(entering, axis, stride, count)
        entering = entering + dot(jump, got)
        if stride * 2 < count:
            got, jump = lax.optimization_barrier((got, jump))
            jump = dot(jump, jump)
        stride *= 2
    return entering


def per_device(fields, conv_in, conv_mid, obs_gain, transition, back_gain, retain):
    bands = lax.axis_size("space")
    blocks = lax.axis_size("tm")
    band = lax.axis_index("space")
    hours = fields.shape[0] // bands
    modes = transition.shape[0]
    gates = retain.reshape(bands, hours, modes)
    transition_t = transition.T

    phis = gates[:, 0, :, None] * transition[None]
    for i in range(1, hours):
        phis = gates[:, i, :, None] * jnp.einsum("ab,sbc->sac", transition, phis, precision=precise)
    block_phi = phis[0]
    for s in range(1, bands):
        block_phi = dot(phis[s], block_phi)

    above = halo(fields, bands)
    above, block_phi = lax.optimization_barrier((above, block_phi))
    partial = encode(fields, above, conv_in, conv_mid, obs_gain, bands)
    increments = sum_bands(partial, bands).reshape(bands, hours, modes)

    state = increments[:, 0]
    local = [state]
    for i in range(1, hours):
        state = gates[:, i] * dot(state, transition_t) + increments[:, i]
        local.append(state)
    local = jnp.stack(local, axis=1)
    ends = local[:, -1]
    block_sum = ends[0]
    for s in range(1, bands):
        block_sum = dot(phis[s], block_sum) + ends[s]

    carry = exclusive_scan(block_phi, block_sum, "tm", blocks)
    starts = [carry]
    for s in range(bands - 1):
        starts.append(dot(phis[s], starts[-1]) + ends[s])
    state = jnp.stack(starts)
    filtered = []
    for i in range(hours):
        state = gates[:, i] * dot(state, transition_t) + increments[:, i]
        filtered.append(state)
    filtered = jnp.stack(filtered, axis=1)

    powers = [jnp.eye(modes, dtype=jnp.float32), back_gain]
    while len(powers) <= hours:
        top = powers[-1]
        more = jnp.einsum("ab,sbc->sac", top, jnp.stack(powers[1:]), precision=precise)
        powers.extend(list(more))
    powers = powers[: hours + 1]
    step = powers[hours]
    joined_t = dot(back_gain, transition).T
    stacked = jnp.concatenate([p.T for p in powers[:hours]], axis=0)
    sources = filtered - jnp.einsum("sia,ab->sib", filtered, joined_t, precision=precise)
    padded = jnp.concatenate([sources, jnp.zeros_like(sources)], axis=1)
    hankel = jnp.concatenate([padded[:, d : d + hours] for d in range(hours)], axis=2)
    inner = dot(hankel.reshape(bands * hours, hours * modes), stacked).reshape(bands, hours, modes)
    heads = inner[:, 0]
    block_head = heads[bands - 1]
    for s in range(bands - 2, -1, -1):
        block_head = heads[s] + dot(step, block_head)
    block_step = step
    reach = 1
    while reach < bands:
        block_step = dot(block_step, block_step)
        reach *= 2

    is_last = lax.axis_index("tm") == blocks - 1
    boundary = dot(transition, filtered[bands - 1, hours - 1])
    block_head = block_head + jnp.where(is_last, dot(block_step, boundary), 0.0)
    entering = suffix_scan(block_head, block_step, "tm", blocks)
    entering = jnp.where(is_last, boundary, entering)

    inputs = [entering]
    for s in range(bands - 1, 0, -1):
        inputs.insert(0, heads[s] + dot(step, inputs[0]))
    mine = lax.dynamic_index_in_dim(jnp.stack(inputs), band, 0, False)
    tails = jnp.concatenate([powers[hours - i].T for i in range(hours)], axis=1)
    smoothed = lax.dynamic_index_in_dim(inner, band, 0, False) + dot(mine[None, :], tails).reshape(hours, modes)
    return lax.dynamic_index_in_dim(filtered, band, 0, False), smoothed


def solution(mesh):
    placed = (
        P("tm", None, "space", None),
        P(),
        P(),
        P("space", None, None, None),
        P(),
        P(),
        P("tm", None),
    )
    return jax.shard_map(
        per_device,
        mesh=mesh,
        in_specs=placed,
        out_specs=(P(FLAT, None), P(FLAT, None)),
        check_vma=False,
    )
```

```python
import jax
import jax.numpy as jnp
from jax import lax
from jax.sharding import PartitionSpec as P

precise = lax.Precision.HIGHEST
FLAT = ("tm", "space")


def dot(a, b):
    return jnp.dot(a, b, precision=precise)


def shift_down(value, axis, steps, count):
    return lax.ppermute(value, axis, [(i, i + steps) for i in range(count - steps)])


def shift_up(value, axis, steps, count):
    return lax.ppermute(value, axis, [(i + steps, i) for i in range(count - steps)])


def conv_stride(images, kernel, layout_out):
    return lax.conv_general_dilated(
        images,
        kernel,
        (2, 2),
        ((0, 0), (1, 1)),
        dimension_numbers=("NCHW", "OIHW", layout_out),
        preferred_element_type=jnp.float32,
    )


def halo(fields, bands):
    return shift_down(fields[:, :, -3:, :], "space", 1, bands)


def encode(fields, above, conv_in, conv_mid, obs_gain, bands):
    band = lax.axis_index("space")
    hidden = conv_stride(jnp.concatenate([above, fields], axis=2), conv_in, "NCHW")
    hidden = jax.nn.silu(hidden).astype(jnp.bfloat16)
    row = lax.broadcasted_iota(jnp.int32, hidden.shape, 2)
    hidden = jnp.where((row == 0) & (band == 0), jnp.zeros_like(hidden), hidden)
    encoded = conv_stride(hidden, conv_mid, "NHWC")
    encoded = jax.nn.silu(encoded).astype(jnp.bfloat16)
    return jnp.einsum("shwc,hwcm->sm", encoded, obs_gain, preferred_element_type=jnp.float32)


def sum_bands(partial, bands):
    got = [lax.ppermute(partial, "space", [(i, (i + d) % bands) for i in range(bands)]) for d in (1, 2, 3)]
    return (partial + got[1]) + (got[2] + got[0])


def exclusive_scan(mats, vecs, axis, count):
    mat1 = shift_down(mats, axis, 1, count)
    mat2 = shift_down(mats, axis, 2, count)
    vec1 = shift_down(vecs, axis, 1, count)
    vec2 = shift_down(vecs, axis, 2, count)
    carry = vec1 + dot(mat1, vec2)
    gain = dot(mat1, mat2)
    stride = 2
    while stride < count:
        more = stride * 2 < count
        got = shift_down(carry, axis, stride, count)
        if more:
            got_gain = shift_down(gain, axis, stride, count)
        carry = carry + dot(gain, got)
        if more:
            gain = dot(gain, got_gain)
        stride *= 2
    return carry


def suffix_scan(heads, step_power, axis, count):
    got1 = shift_up(heads, axis, 1, count)
    got2 = shift_up(heads, axis, 2, count)
    entering = got1 + dot(step_power, got2)
    jump = dot(step_power, step_power)
    stride = 2
    while stride < count:
        got = shift_up(entering, axis, stride, count)
        entering = entering + dot(jump, got)
        if stride * 2 < count:
            jump = dot(jump, jump)
        stride *= 2
    return entering


def per_device(fields, conv_in, conv_mid, obs_gain, transition, back_gain, retain):
    bands = lax.axis_size("space")
    blocks = lax.axis_size("tm")
    band = lax.axis_index("space")
    hours = fields.shape[0] // bands
    modes = transition.shape[0]
    gates = retain.reshape(bands, hours, modes)
    transition_t = transition.T

    phis = gates[:, 0, :, None] * transition[None]
    for i in range(1, hours):
        phis = gates[:, i, :, None] * jnp.einsum("ab,sbc->sac", transition, phis, precision=precise)
    block_phi = phis[0]
    for s in range(1, bands):
        block_phi = dot(phis[s], block_phi)

    above = halo(fields, bands)
    above, block_phi = lax.optimization_barrier((above, block_phi))
    partial = encode(fields, above, conv_in, conv_mid, obs_gain, bands)
    increments = sum_bands(partial, bands).reshape(bands, hours, modes)

    gate_cols = jnp.transpose(gates, (1, 2, 0))
    step_cols = jnp.transpose(increments, (1, 2, 0))
    state = step_cols[0]
    for i in range(1, hours):
        state = gate_cols[i] * dot(transition, state) + step_cols[i]
    ends = state.T
    block_sum = ends[0]
    for s in range(1, bands):
        block_sum = dot(phis[s], block_sum) + ends[s]

    carry = exclusive_scan(block_phi, block_sum, "tm", blocks)
    starts = [carry]
    for s in range(bands - 1):
        starts.append(dot(phis[s], starts[-1]) + ends[s])
    state = jnp.stack(starts).T
    filtered = []
    for i in range(hours):
        state = gate_cols[i] * dot(transition, state) + step_cols[i]
        filtered.append(state)
    filtered = jnp.transpose(jnp.stack(filtered), (2, 0, 1))

    powers = [jnp.eye(modes, dtype=jnp.float32), back_gain]
    while len(powers) <= hours:
        top = powers[-1]
        more = jnp.einsum("ab,sbc->sac", top, jnp.stack(powers[1:]), precision=precise)
        powers.extend(list(more))
    powers = powers[: hours + 1]
    step = powers[hours]
    joined_t = dot(back_gain, transition).T
    stacked = jnp.concatenate([p.T for p in powers[:hours]], axis=0)
    sources = filtered - jnp.einsum("sia,ab->sib", filtered, joined_t, precision=precise)
    padded = jnp.concatenate([sources, jnp.zeros_like(sources)], axis=1)
    hankel = jnp.concatenate([padded[:, d : d + hours] for d in range(hours)], axis=2)
    inner = dot(hankel.reshape(bands * hours, hours * modes), stacked).reshape(bands, hours, modes)
    heads = inner[:, 0]
    block_head = heads[bands - 1]
    for s in range(bands - 2, -1, -1):
        block_head = heads[s] + dot(step, block_head)
    block_step = step
    reach = 1
    while reach < bands:
        block_step = dot(block_step, block_step)
        reach *= 2

    is_last = lax.axis_index("tm") == blocks - 1
    boundary = dot(transition, filtered[bands - 1, hours - 1])
    block_head = block_head + jnp.where(is_last, dot(block_step, boundary), 0.0)
    entering = suffix_scan(block_head, block_step, "tm", blocks)
    entering = jnp.where(is_last, boundary, entering)

    inputs = [entering]
    for s in range(bands - 1, 0, -1):
        inputs.insert(0, heads[s] + dot(step, inputs[0]))
    mine = lax.dynamic_index_in_dim(jnp.stack(inputs), band, 0, False)
    tails = jnp.concatenate([powers[hours - i].T for i in range(hours)], axis=1)
    smoothed = lax.dynamic_index_in_dim(inner, band, 0, False) + dot(mine[None, :], tails).reshape(hours, modes)
    return lax.dynamic_index_in_dim(filtered, band, 0, False), smoothed


def solution(mesh):
    placed = (
        P("tm", None, "space", None),
        P(),
        P(),
        P("space", None, None, None),
        P(),
        P(),
        P("tm", None),
    )
    return jax.shard_map(
        per_device,
        mesh=mesh,
        in_specs=placed,
        out_specs=(P(FLAT, None), P(FLAT, None)),
        check_vma=False,
    )
```

```python
import jax
import jax.numpy as jnp
from jax import lax
from jax.sharding import PartitionSpec as P

precise = lax.Precision.HIGHEST
FLAT = ("tm", "space")


def dot(a, b):
    return jnp.dot(a, b, precision=precise)


def shift_down(value, axis, steps, count):
    return lax.ppermute(value, axis, [(i, i + steps) for i in range(count - steps)])


def shift_up(value, axis, steps, count):
    return lax.ppermute(value, axis, [(i + steps, i) for i in range(count - steps)])


def conv_stride(images, kernel, layout_out):
    return lax.conv_general_dilated(
        images,
        kernel,
        (2, 2),
        ((0, 0), (1, 1)),
        dimension_numbers=("NCHW", "OIHW", layout_out),
        preferred_element_type=jnp.float32,
    )


def halo(fields, bands):
    return shift_down(fields[:, :, -3:, :], "space", 1, bands)


def encode(fields, above, conv_in, conv_mid, obs_gain, bands):
    band = lax.axis_index("space")
    hidden = conv_stride(jnp.concatenate([above, fields], axis=2), conv_in, "NCHW")
    hidden = jax.nn.silu(hidden).astype(jnp.bfloat16)
    row = lax.broadcasted_iota(jnp.int32, hidden.shape, 2)
    hidden = jnp.where((row == 0) & (band == 0), jnp.zeros_like(hidden), hidden)
    encoded = conv_stride(hidden, conv_mid, "NHWC")
    encoded = jax.nn.silu(encoded).astype(jnp.bfloat16)
    return jnp.einsum("shwc,hwcm->sm", encoded, obs_gain, preferred_element_type=jnp.float32)


def sum_bands(partial, bands):
    got = [lax.ppermute(partial, "space", [(i, (i + d) % bands) for i in range(bands)]) for d in (1, 2, 3)]
    return (partial + got[1]) + (got[2] + got[0])


def exclusive_scan(mats, vecs, axis, count):
    mat1 = shift_down(mats, axis, 1, count)
    mat2 = shift_down(mats, axis, 2, count)
    vec1 = shift_down(vecs, axis, 1, count)
    vec2 = shift_down(vecs, axis, 2, count)
    carry = vec1 + dot(mat1, vec2)
    gain = dot(mat1, mat2)
    stride = 2
    while stride < count:
        more = stride * 2 < count
        got = shift_down(carry, axis, stride, count)
        if more:
            got_gain = shift_down(gain, axis, stride, count)
        carry = carry + dot(gain, got)
        if more:
            gain = dot(gain, got_gain)
        stride *= 2
    return carry


def suffix_scan(heads, step_power, axis, count):
    got1 = shift_up(heads, axis, 1, count)
    got2 = shift_up(heads, axis, 2, count)
    entering = got1 + dot(step_power, got2)
    jump = dot(step_power, step_power)
    stride = 2
    while stride < count:
        got = shift_up(entering, axis, stride, count)
        entering = entering + dot(jump, got)
        if stride * 2 < count:
            jump = dot(jump, jump)
        stride *= 2
    return entering


def per_device(fields, conv_in, conv_mid, obs_gain, transition, back_gain, retain):
    bands = lax.axis_size("space")
    blocks = lax.axis_size("tm")
    band = lax.axis_index("space")
    hours = fields.shape[0] // bands
    modes = transition.shape[0]
    gates = retain.reshape(bands, hours, modes)
    transition_t = transition.T

    phis = gates[:, 0, :, None] * transition[None]
    for i in range(1, hours):
        phis = gates[:, i, :, None] * jnp.einsum("ab,sbc->sac", transition, phis, precision=lax.Precision.HIGH)
    block_phi = phis[0]
    for s in range(1, bands):
        block_phi = dot(phis[s], block_phi)

    above = halo(fields, bands)
    above, block_phi = lax.optimization_barrier((above, block_phi))
    partial = encode(fields, above, conv_in, conv_mid, obs_gain, bands)
    increments = sum_bands(partial, bands).reshape(bands, hours, modes)

    gate_cols = jnp.transpose(gates, (1, 2, 0))
    step_cols = jnp.transpose(increments, (1, 2, 0))
    state = step_cols[0]
    for i in range(1, hours):
        state = gate_cols[i] * dot(transition, state) + step_cols[i]
    ends = state.T
    block_sum = ends[0]
    for s in range(1, bands):
        block_sum = dot(phis[s], block_sum) + ends[s]

    carry = exclusive_scan(block_phi, block_sum, "tm", blocks)
    starts = [carry]
    for s in range(bands - 1):
        starts.append(dot(phis[s], starts[-1]) + ends[s])
    state = jnp.stack(starts).T
    filtered = []
    for i in range(hours):
        state = gate_cols[i] * dot(transition, state) + step_cols[i]
        filtered.append(state)
    filtered = jnp.transpose(jnp.stack(filtered), (2, 0, 1))

    powers = [jnp.eye(modes, dtype=jnp.float32), back_gain]
    while len(powers) <= hours:
        top = powers[-1]
        more = jnp.einsum("ab,sbc->sac", top, jnp.stack(powers[1:]), precision=precise)
        powers.extend(list(more))
    powers = powers[: hours + 1]
    step = powers[hours]
    joined_t = dot(back_gain, transition).T
    stacked = jnp.concatenate([p.T for p in powers[:hours]], axis=0)
    sources = filtered - jnp.einsum("sia,ab->sib", filtered, joined_t, precision=precise)
    padded = jnp.concatenate([sources, jnp.zeros_like(sources)], axis=1)
    hankel = jnp.concatenate([padded[:, d : d + hours] for d in range(hours)], axis=2)
    inner = dot(hankel.reshape(bands * hours, hours * modes), stacked).reshape(bands, hours, modes)
    heads = inner[:, 0]
    block_head = heads[bands - 1]
    for s in range(bands - 2, -1, -1):
        block_head = heads[s] + dot(step, block_head)
    block_step = step
    reach = 1
    while reach < bands:
        block_step = dot(block_step, block_step)
        reach *= 2

    is_last = lax.axis_index("tm") == blocks - 1
    boundary = dot(transition, filtered[bands - 1, hours - 1])
    block_head = block_head + jnp.where(is_last, dot(block_step, boundary), 0.0)
    entering = suffix_scan(block_head, block_step, "tm", blocks)
    entering = jnp.where(is_last, boundary, entering)

    inputs = [entering]
    for s in range(bands - 1, 0, -1):
        inputs.insert(0, heads[s] + dot(step, inputs[0]))
    mine = lax.dynamic_index_in_dim(jnp.stack(inputs), band, 0, False)
    tails = jnp.concatenate([powers[hours - i].T for i in range(hours)], axis=1)
    smoothed = lax.dynamic_index_in_dim(inner, band, 0, False) + dot(mine[None, :], tails).reshape(hours, modes)
    return lax.dynamic_index_in_dim(filtered, band, 0, False), smoothed


def solution(mesh):
    placed = (
        P("tm", None, "space", None),
        P(),
        P(),
        P("space", None, None, None),
        P(),
        P(),
        P("tm", None),
    )
    return jax.shard_map(
        per_device,
        mesh=mesh,
        in_specs=placed,
        out_specs=(P(FLAT, None), P(FLAT, None)),
        check_vma=False,
    )
```

```python
import jax
import jax.numpy as jnp
from jax import lax
from jax.sharding import PartitionSpec as P

precise = lax.Precision.HIGHEST
FLAT = ("tm", "space")


def dot(a, b):
    return jnp.dot(a, b, precision=precise)


def shift_down(value, axis, steps, count):
    return lax.ppermute(value, axis, [(i, i + steps) for i in range(count - steps)])


def shift_up(value, axis, steps, count):
    return lax.ppermute(value, axis, [(i + steps, i) for i in range(count - steps)])


def conv_stride(images, kernel, layout_out):
    return lax.conv_general_dilated(
        images,
        kernel,
        (2, 2),
        ((0, 0), (1, 1)),
        dimension_numbers=("NCHW", "OIHW", layout_out),
        preferred_element_type=jnp.float32,
    )


def halo(fields, bands):
    return shift_down(fields[:, :, -3:, :], "space", 1, bands)


def encode(fields, above, conv_in, conv_mid, obs_gain, bands):
    band = lax.axis_index("space")
    hidden = conv_stride(jnp.concatenate([above, fields], axis=2), conv_in, "NCHW")
    hidden = jax.nn.silu(hidden).astype(jnp.bfloat16)
    row = lax.broadcasted_iota(jnp.int32, hidden.shape, 2)
    hidden = jnp.where((row == 0) & (band == 0), jnp.zeros_like(hidden), hidden)
    encoded = conv_stride(hidden, conv_mid, "NHWC")
    encoded = jax.nn.silu(encoded).astype(jnp.bfloat16)
    return jnp.einsum("shwc,hwcm->sm", encoded, obs_gain, preferred_element_type=jnp.float32)


def sum_bands(partial, bands):
    got = [lax.ppermute(partial, "space", [(i, (i + d) % bands) for i in range(bands)]) for d in (1, 2, 3)]
    return (partial + got[1]) + (got[2] + got[0])


def exclusive_scan(mats, vecs, axis, count):
    mat1 = shift_down(mats, axis, 1, count)
    mat2 = shift_down(mats, axis, 2, count)
    vec1 = shift_down(vecs, axis, 1, count)
    vec2 = shift_down(vecs, axis, 2, count)
    carry = vec1 + dot(mat1, vec2)
    gain = dot(mat1, mat2)
    stride = 2
    while stride < count:
        more = stride * 2 < count
        got = shift_down(carry, axis, stride, count)
        if more:
            got_gain = shift_down(gain, axis, stride, count)
        carry = carry + dot(gain, got)
        if more:
            gain = dot(gain, got_gain)
        stride *= 2
    return carry


def suffix_scan(heads, step_power, axis, count):
    got1 = shift_up(heads, axis, 1, count)
    got2 = shift_up(heads, axis, 2, count)
    entering = got1 + dot(step_power, got2)
    jump = dot(step_power, step_power)
    stride = 2
    while stride < count:
        got = shift_up(entering, axis, stride, count)
        entering = entering + dot(jump, got)
        if stride * 2 < count:
            jump = dot(jump, jump)
        stride *= 2
    return entering


def per_device(fields, conv_in, conv_mid, obs_gain, transition, back_gain, retain):
    bands = lax.axis_size("space")
    blocks = lax.axis_size("tm")
    band = lax.axis_index("space")
    hours = fields.shape[0] // bands
    modes = transition.shape[0]
    gates = retain.reshape(bands, hours, modes)
    transition_t = transition.T

    phis = gates[:, 0, :, None] * transition[None]
    for i in range(1, hours):
        phis = gates[:, i, :, None] * jnp.einsum("ab,sbc->sac", transition, phis, precision=precise)
    block_phi = phis[0]
    for s in range(1, bands):
        block_phi = dot(phis[s], block_phi)

    above = halo(fields, bands)
    above, block_phi = lax.optimization_barrier((above, block_phi))
    partial = encode(fields, above, conv_in, conv_mid, obs_gain, bands)
    increments = sum_bands(partial, bands).reshape(bands, hours, modes)

    gate_cols = jnp.transpose(gates, (1, 2, 0))
    step_cols = jnp.transpose(increments, (1, 2, 0))
    state = step_cols[0]
    for i in range(1, hours):
        state = gate_cols[i] * dot(transition, state) + step_cols[i]
    ends = state.T
    block_sum = ends[0]
    for s in range(1, bands):
        block_sum = dot(phis[s], block_sum) + ends[s]

    carry = exclusive_scan(block_phi, block_sum, "tm", blocks)
    starts = [carry]
    for s in range(bands - 1):
        starts.append(dot(phis[s], starts[-1]) + ends[s])
    state = jnp.stack(starts).T
    filtered = []
    for i in range(hours):
        state = gate_cols[i] * dot(transition, state) + step_cols[i]
        filtered.append(state)
    filtered = jnp.transpose(jnp.stack(filtered), (2, 0, 1))

    powers = [jnp.eye(modes, dtype=jnp.float32), back_gain]
    while len(powers) <= hours:
        top = powers[-1]
        more = jnp.einsum("ab,sbc->sac", top, jnp.stack(powers[1:]), precision=precise)
        powers.extend(list(more))
    powers = powers[: hours + 1]
    step = powers[hours]
    joined_t = dot(back_gain, transition).T
    stacked = jnp.stack(powers[:hours])
    sources = filtered - jnp.einsum("sia,ab->sib", filtered, joined_t, precision=precise)
    padded = jnp.concatenate([sources, jnp.zeros_like(sources)], axis=1)
    hankel = jnp.stack([padded[:, d : d + hours] for d in range(hours)], axis=2)
    inner = jnp.einsum("sidb,dab->sia", hankel, stacked, precision=precise)
    heads = inner[:, 0]
    block_head = heads[bands - 1]
    for s in range(bands - 2, -1, -1):
        block_head = heads[s] + dot(step, block_head)
    block_step = step
    reach = 1
    while reach < bands:
        block_step = dot(block_step, block_step)
        reach *= 2

    is_last = lax.axis_index("tm") == blocks - 1
    boundary = dot(transition, filtered[bands - 1, hours - 1])
    block_head = block_head + jnp.where(is_last, dot(block_step, boundary), 0.0)
    entering = suffix_scan(block_head, block_step, "tm", blocks)
    entering = jnp.where(is_last, boundary, entering)

    inputs = [entering]
    for s in range(bands - 1, 0, -1):
        inputs.insert(0, heads[s] + dot(step, inputs[0]))
    mine = lax.dynamic_index_in_dim(jnp.stack(inputs), band, 0, False)
    tails = jnp.stack([powers[hours - i] for i in range(hours)])
    smoothed = lax.dynamic_index_in_dim(inner, band, 0, False) + jnp.einsum("iab,b->ia", tails, mine, precision=precise)
    return lax.dynamic_index_in_dim(filtered, band, 0, False), smoothed


def solution(mesh):
    placed = (
        P("tm", None, "space", None),
        P(),
        P(),
        P("space", None, None, None),
        P(),
        P(),
        P("tm", None),
    )
    return jax.shard_map(
        per_device,
        mesh=mesh,
        in_specs=placed,
        out_specs=(P(FLAT, None), P(FLAT, None)),
        check_vma=False,
    )
```

```python
import jax
import jax.numpy as jnp
from jax import lax
from jax.sharding import PartitionSpec as P

precise = lax.Precision.HIGHEST
FLAT = ("tm", "space")


def dot(a, b):
    return jnp.dot(a, b, precision=precise)


def shift_down(value, axis, steps, count):
    return lax.ppermute(value, axis, [(i, i + steps) for i in range(count - steps)])


def shift_up(value, axis, steps, count):
    return lax.ppermute(value, axis, [(i + steps, i) for i in range(count - steps)])


def conv_stride(images, kernel, layout_out):
    return lax.conv_general_dilated(
        images,
        kernel,
        (2, 2),
        ((0, 0), (1, 1)),
        dimension_numbers=("NCHW", "OIHW", layout_out),
        preferred_element_type=jnp.float32,
    )


def halo(fields, bands):
    return shift_down(fields[:, :, -3:, :], "space", 1, bands)


def encode(fields, above, conv_in, conv_mid, obs_gain, bands):
    band = lax.axis_index("space")
    hidden = conv_stride(jnp.concatenate([above, fields], axis=2), conv_in, "NCHW")
    hidden = jax.nn.silu(hidden).astype(jnp.bfloat16)
    row = lax.broadcasted_iota(jnp.int32, hidden.shape, 2)
    hidden = jnp.where((row == 0) & (band == 0), jnp.zeros_like(hidden), hidden)
    encoded = conv_stride(hidden, conv_mid, "NHWC")
    encoded = jax.nn.silu(encoded).astype(jnp.bfloat16)
    return jnp.einsum("shwc,hwcm->sm", encoded, obs_gain, preferred_element_type=jnp.float32)


def sum_bands(partial, bands):
    got = [lax.ppermute(partial, "space", [(i, (i + d) % bands) for i in range(bands)]) for d in (1, 2, 3)]
    return (partial + got[1]) + (got[2] + got[0])


def exclusive_scan(mats, vecs, axis, count):
    mat1 = shift_down(mats, axis, 1, count)
    mat2 = shift_down(mats, axis, 2, count)
    vec1 = shift_down(vecs, axis, 1, count)
    vec2 = shift_down(vecs, axis, 2, count)
    carry = vec1 + dot(mat1, vec2)
    gain = dot(mat1, mat2)
    stride = 2
    while stride < count:
        more = stride * 2 < count
        got = shift_down(carry, axis, stride, count)
        if more:
            got_gain = shift_down(gain, axis, stride, count)
        carry = carry + dot(gain, got)
        if more:
            gain = dot(gain, got_gain)
        stride *= 2
    return carry


def suffix_scan(heads, step_power, axis, count):
    got1 = shift_up(heads, axis, 1, count)
    got2 = shift_up(heads, axis, 2, count)
    entering = got1 + dot(step_power, got2)
    jump = dot(step_power, step_power)
    stride = 2
    while stride < count:
        got = shift_up(entering, axis, stride, count)
        entering = entering + dot(jump, got)
        if stride * 2 < count:
            jump = dot(jump, jump)
        stride *= 2
    return entering


def per_device(fields, conv_in, conv_mid, obs_gain, transition, back_gain, retain):
    bands = lax.axis_size("space")
    blocks = lax.axis_size("tm")
    band = lax.axis_index("space")
    hours = fields.shape[0] // bands
    modes = transition.shape[0]
    gates = retain.reshape(bands, hours, modes)
    transition_t = transition.T

    phis = gates[:, 0, :, None] * transition[None]
    for i in range(1, hours):
        phis = gates[:, i, :, None] * jnp.einsum("ab,sbc->sac", transition, phis, precision=precise)
    block_phi = phis[0]
    for s in range(1, bands):
        block_phi = dot(phis[s], block_phi)

    above = halo(fields, bands)
    above, block_phi = lax.optimization_barrier((above, block_phi))
    partial = encode(fields, above, conv_in, conv_mid, obs_gain, bands)
    increments = sum_bands(partial, bands).reshape(bands, hours, modes)

    gate_cols = jnp.transpose(gates, (1, 2, 0))
    step_cols = jnp.transpose(increments, (1, 2, 0))
    state = step_cols[0]
    for i in range(1, hours):
        state = gate_cols[i] * dot(transition, state) + step_cols[i]
    ends = state.T
    block_sum = ends[0]
    for s in range(1, bands):
        block_sum = dot(phis[s], block_sum) + ends[s]

    carry = exclusive_scan(block_phi, block_sum, "tm", blocks)
    starts = [carry]
    for s in range(bands - 1):
        starts.append(dot(phis[s], starts[-1]) + ends[s])
    state = jnp.stack(starts).T
    filtered = []
    for i in range(hours):
        state = gate_cols[i] * dot(transition, state) + step_cols[i]
        filtered.append(state)
    filtered = jnp.transpose(jnp.stack(filtered), (2, 0, 1))

    powers = [jnp.eye(modes, dtype=jnp.float32), back_gain]
    while len(powers) <= hours:
        top = powers[-1]
        more = jnp.einsum("ab,sbc->sac", top, jnp.stack(powers[1:]), precision=precise)
        powers.extend(list(more))
    powers = powers[: hours + 1]
    step = powers[hours]
    joined_t = dot(back_gain, transition).T
    every = jnp.stack(powers[: hours + 1])
    stacked = every[:hours]
    sources = filtered - jnp.einsum("sia,ab->sib", filtered, joined_t, precision=precise)
    padded = jnp.concatenate([sources, jnp.zeros_like(sources)], axis=1)
    hankel = jnp.stack([padded[:, d : d + hours] for d in range(hours)], axis=2)
    inner = jnp.einsum("sidb,dab->sia", hankel, stacked, precision=precise)
    heads = inner[:, 0]
    block_head = heads[bands - 1]
    for s in range(bands - 2, -1, -1):
        block_head = heads[s] + dot(step, block_head)
    block_step = step
    reach = 1
    while reach < bands:
        block_step = dot(block_step, block_step)
        reach *= 2

    is_last = lax.axis_index("tm") == blocks - 1
    boundary = dot(transition, filtered[bands - 1, hours - 1])
    block_head = block_head + jnp.where(is_last, dot(block_step, boundary), 0.0)
    entering = suffix_scan(block_head, block_step, "tm", blocks)
    entering = jnp.where(is_last, boundary, entering)

    inputs = [entering]
    for s in range(bands - 1, 0, -1):
        inputs.insert(0, heads[s] + dot(step, inputs[0]))
    mine = lax.dynamic_index_in_dim(jnp.stack(inputs), band, 0, False)
    reached = jnp.einsum("jab,b->ja", every[1:], mine, precision=precise)[::-1]
    smoothed = lax.dynamic_index_in_dim(inner, band, 0, False) + reached
    return lax.dynamic_index_in_dim(filtered, band, 0, False), smoothed


def solution(mesh):
    placed = (
        P("tm", None, "space", None),
        P(),
        P(),
        P("space", None, None, None),
        P(),
        P(),
        P("tm", None),
    )
    return jax.shard_map(
        per_device,
        mesh=mesh,
        in_specs=placed,
        out_specs=(P(FLAT, None), P(FLAT, None)),
        check_vma=False,
    )
```

```python
import jax
import jax.numpy as jnp
from jax import lax
from jax.sharding import PartitionSpec as P

precise = lax.Precision.HIGHEST
FLAT = ("tm", "space")


def dot(a, b):
    return jnp.dot(a, b, precision=precise)


def shift_down(value, axis, steps, count):
    return lax.ppermute(value, axis, [(i, i + steps) for i in range(count - steps)])


def shift_up(value, axis, steps, count):
    return lax.ppermute(value, axis, [(i + steps, i) for i in range(count - steps)])


def conv_stride(images, kernel, layout_out):
    return lax.conv_general_dilated(
        images,
        kernel,
        (2, 2),
        ((0, 0), (1, 1)),
        dimension_numbers=("NCHW", "OIHW", layout_out),
        preferred_element_type=jnp.float32,
    )


def halo(fields, bands):
    return shift_down(fields[:, :, -3:, :], "space", 1, bands)


def encode(fields, above, conv_in, conv_mid, obs_gain, bands):
    band = lax.axis_index("space")
    hidden = conv_stride(jnp.concatenate([above, fields], axis=2), conv_in, "NCHW")
    hidden = jax.nn.silu(hidden).astype(jnp.bfloat16)
    row = lax.broadcasted_iota(jnp.int32, hidden.shape, 2)
    hidden = jnp.where((row == 0) & (band == 0), jnp.zeros_like(hidden), hidden)
    encoded = conv_stride(hidden, conv_mid, "NHWC")
    encoded = jax.nn.silu(encoded).astype(jnp.bfloat16)
    return jnp.einsum("shwc,hwcm->sm", encoded, obs_gain, preferred_element_type=jnp.float32)


def sum_bands(partial, bands):
    got = [lax.ppermute(partial, "space", [(i, (i + d) % bands) for i in range(bands)]) for d in (1, 2, 3)]
    return (partial + got[1]) + (got[2] + got[0])


def exclusive_scan(mats, vecs, axis, count):
    mat1 = shift_down(mats, axis, 1, count)
    mat2 = shift_down(mats, axis, 2, count)
    vec1 = shift_down(vecs, axis, 1, count)
    vec2 = shift_down(vecs, axis, 2, count)
    carry = vec1 + dot(mat1, vec2)
    gain = dot(mat1, mat2)
    stride = 2
    while stride < count:
        more = stride * 2 < count
        got = shift_down(carry, axis, stride, count)
        if more:
            got_gain = shift_down(gain, axis, stride, count)
        carry = carry + dot(gain, got)
        if more:
            gain = dot(gain, got_gain)
        stride *= 2
    return carry


def suffix_scan(heads, step_power, axis, count):
    got1 = shift_up(heads, axis, 1, count)
    got2 = shift_up(heads, axis, 2, count)
    entering = got1 + dot(step_power, got2)
    jump = dot(step_power, step_power)
    stride = 2
    while stride < count:
        got = shift_up(entering, axis, stride, count)
        entering = entering + dot(jump, got)
        if stride * 2 < count:
            jump = dot(jump, jump)
        stride *= 2
    return entering


def per_device(fields, conv_in, conv_mid, obs_gain, transition, back_gain, retain):
    bands = lax.axis_size("space")
    blocks = lax.axis_size("tm")
    band = lax.axis_index("space")
    hours = fields.shape[0] // bands
    modes = transition.shape[0]
    gates = retain.reshape(bands, hours, modes)
    transition_t = transition.T

    phis = gates[:, 0, :, None] * transition[None]
    for i in range(1, hours):
        phis = gates[:, i, :, None] * jnp.einsum("ab,sbc->sac", transition, phis, precision=precise)
    block_phi = phis[0]
    leading = [jnp.eye(modes, dtype=jnp.float32), block_phi]
    for s in range(1, bands):
        block_phi = dot(phis[s], block_phi)
        leading.append(block_phi)
    leading = jnp.stack(leading[:bands])

    above = halo(fields, bands)
    above, block_phi = lax.optimization_barrier((above, block_phi))
    partial = encode(fields, above, conv_in, conv_mid, obs_gain, bands)
    increments = sum_bands(partial, bands).reshape(bands, hours, modes)

    gate_cols = jnp.transpose(gates, (1, 2, 0))
    step_cols = jnp.transpose(increments, (1, 2, 0))
    state = step_cols[0]
    for i in range(1, hours):
        state = gate_cols[i] * dot(transition, state) + step_cols[i]
    ends = state.T
    block_sum = ends[0]
    for s in range(1, bands):
        block_sum = dot(phis[s], block_sum) + ends[s]

    offsets = [jnp.zeros_like(ends[0])]
    for s in range(bands - 1):
        offsets.append(dot(phis[s], offsets[-1]) + ends[s])
    carry = exclusive_scan(block_phi, block_sum, "tm", blocks)
    state = (jnp.einsum("sab,b->sa", leading, carry, precision=precise) + jnp.stack(offsets)).T
    filtered = []
    for i in range(hours):
        state = gate_cols[i] * dot(transition, state) + step_cols[i]
        filtered.append(state)
    filtered = jnp.transpose(jnp.stack(filtered), (2, 0, 1))

    powers = [jnp.eye(modes, dtype=jnp.float32), back_gain]
    while len(powers) <= hours:
        top = powers[-1]
        more = jnp.einsum("ab,sbc->sac", top, jnp.stack(powers[1:]), precision=precise)
        powers.extend(list(more))
    powers = powers[: hours + 1]
    step = powers[hours]
    joined_t = dot(back_gain, transition).T
    every = jnp.stack(powers[: hours + 1])
    stacked = every[:hours]
    sources = filtered - jnp.einsum("sia,ab->sib", filtered, joined_t, precision=precise)
    padded = jnp.concatenate([sources, jnp.zeros_like(sources)], axis=1)
    hankel = jnp.stack([padded[:, d : d + hours] for d in range(hours)], axis=2)
    inner = jnp.einsum("sidb,dab->sia", hankel, stacked, precision=precise)
    heads = inner[:, 0]
    block_head = heads[bands - 1]
    for s in range(bands - 2, -1, -1):
        block_head = heads[s] + dot(step, block_head)
    block_step = step
    reach = 1
    while reach < bands:
        block_step = dot(block_step, block_step)
        reach *= 2

    is_last = lax.axis_index("tm") == blocks - 1
    boundary = dot(transition, filtered[bands - 1, hours - 1])
    block_head = block_head + jnp.where(is_last, dot(block_step, boundary), 0.0)
    entering = suffix_scan(block_head, block_step, "tm", blocks)
    entering = jnp.where(is_last, boundary, entering)

    inputs = [entering]
    for s in range(bands - 1, 0, -1):
        inputs.insert(0, heads[s] + dot(step, inputs[0]))
    mine = lax.dynamic_index_in_dim(jnp.stack(inputs), band, 0, False)
    reached = jnp.einsum("jab,b->ja", every[1:], mine, precision=precise)[::-1]
    smoothed = lax.dynamic_index_in_dim(inner, band, 0, False) + reached
    return lax.dynamic_index_in_dim(filtered, band, 0, False), smoothed


def solution(mesh):
    placed = (
        P("tm", None, "space", None),
        P(),
        P(),
        P("space", None, None, None),
        P(),
        P(),
        P("tm", None),
    )
    return jax.shard_map(
        per_device,
        mesh=mesh,
        in_specs=placed,
        out_specs=(P(FLAT, None), P(FLAT, None)),
        check_vma=False,
    )
```
